32 devices in a mesh: groups: 2 (over y), tile: 4 (over z), depth: 2 (over x), wave: 2 (over core).
Axes of the slice: x: 2, y: 2, z: 4, core: 2. Of those that a mesh axis runs over, the one named last changes fastest.
Arguments:
- incident: float32 [3, 2, 512, 256], P(None, None, ('groups', 'tile'), 'wave'), parts along dimension 2, may hold values from -6 to 6
- phase_shift: bfloat16 [8, 512, 256], P('depth', ('groups', 'tile'), 'wave'), parts along dimension 1, may hold values from -3.140625 to 3.140625
- absorption: bfloat16 [8, 512, 256], P('depth', ('groups', 'tile'), 'wave'), parts along dimension 1, may hold values from 0 to 0.059814453
- fir_taps: float32 [2, 33], replicated, may hold values from -0.6 to 0.6
Outputs:
- exit_waves: float32 [2, 3, 2, 512, 256], P('depth', None, None, ('groups', 'tile'), 'wave'), parts along dimension 3
The draws below stay inside these ranges and needn't reach their ends.
There are 2 independent parts, one for each index of `groups`. The reference program is written for one: setup_inputs(seed, part) draws one part's arguments, and reference() takes and returns one part's arrays. A program takes and returns all parts, laid end to end along the dimension named above; an argument that names none is the same for every part. Nothing has to cross between parts.
All inputs are finite; a program needn't handle non-finite values.
Results may differ from the reference program's by a relative error of at most 0.0003.
Values may be sent and summed in bfloat16 or wider, within the bound.
No kernel may reach another device: no remote copies, remote signals or barrier semaphores. Data moves between devices by JAX's collectives and lax.ppermute only.
A program may use at most 64 MiB of HBM per device.

```python
import jax
import jax.numpy as jnp
from jax import lax

ILLUM = 3
SL_DEV = 4
TAPS = 33
HALF = 16
SLICES = 8
NX = 256
NY = 256
N_DEPTH = 2


def steps_of(stream_key, shape, shards, low, top_value):
    gain, own = 1.0, jax.random.fold_in(stream_key, 6)
    for dim, shards_of in shards:
        draws = jnp.exp(jax.random.uniform(jax.random.fold_in(own, dim), (shards_of,), jnp.float32, low / len(shards), top_value / len(shards)))
        gain = gain * jnp.repeat(draws, shape[dim] // shards_of).reshape([-1 if axis == dim else 1 for axis in range(len(shape))])
    return gain


def gaussian(rng, extent, scale, reach, pieces=(), dtype=jnp.bfloat16):
    values = scale * jax.random.normal(rng, extent, jnp.float32)
    if pieces:
        values = values * steps_of(rng, extent, pieces, -0.22, 0.18)
    return jnp.clip(values, -reach, reach).astype(dtype)


def setup_inputs(seed: int = 0, part: int = 0) -> dict:
    streams_of = jax.random.split(jax.random.key(seed), 5)
    own_keys = jax.random.split(jax.random.fold_in(streams_of[4], part), 5)
    incident = gaussian(own_keys[0], (ILLUM, 2, NX, NY), 1.0, 6.0, ((2, 4), (3, 2)), jnp.float32)
    phase_shift = jnp.clip(jax.random.uniform(own_keys[1], (SLICES, NX, NY), jnp.float32, -3.140625, 3.140625), -3.140625, 3.140625).astype(jnp.bfloat16)
    absorption = jnp.clip(0.059814453 * jax.random.uniform(own_keys[2], (SLICES, NX, NY), jnp.float32) ** steps_of(own_keys[2], (SLICES, NX, NY), ((0, 2), (1, 4), (2, 2)), -0.2, 0.2), 0.0, 0.059814453).astype(jnp.bfloat16)
    fir_taps = gaussian(streams_of[3], (2, TAPS), 0.13, 0.6, (), jnp.float32)
    return dict(incident=incident, phase_shift=phase_shift, absorption=absorption, fir_taps=fir_taps)


def apply_taps(field, kernel, axis):
    real_part = field[:, 0]
    imag_part = field[:, 1]
    sub_axis = axis - 1
    length = field.shape[axis] - 2 * HALF
    sum_real = jnp.zeros(real_part.shape[:sub_axis] + (length,) + real_part.shape[sub_axis + 1:], jnp.float32)
    sum_imag = jnp.zeros_like(sum_real)
    for layer in range(TAPS):
        shifted_real = lax.slice_in_dim(real_part, layer, layer + length, axis=sub_axis)
        shifted_imag = lax.slice_in_dim(imag_part, layer, layer + length, axis=sub_axis)
        tap_real = kernel[0, layer]
        tap_imag = kernel[1, layer]
        sum_real = sum_real + tap_real * shifted_real - tap_imag * shifted_imag
        sum_imag = sum_imag + tap_real * shifted_imag + tap_imag * shifted_real
    return jnp.stack([sum_real, sum_imag], axis=1)

def transmission(phase_part, absorb_part):
    amplitude = jnp.exp(-absorb_part.astype(jnp.float32))
    angle_part = phase_part.astype(jnp.float32)
    return jnp.stack([amplitude * jnp.cos(angle_part), amplitude * jnp.sin(angle_part)], axis=-3)

def modulate(field, trans):
    field_real = field[:, 0]
    field_imag = field[:, 1]
    return jnp.stack([field_real * trans[0] - field_imag * trans[1], field_real * trans[1] + field_imag * trans[0]], axis=1)

def reference(incident, phase_shift, absorption, fir_taps):
    kernel = fir_taps / jnp.sqrt(jnp.sum(fir_taps * fir_taps) + 1e-06)
    phase_groups = phase_shift.reshape(N_DEPTH, SL_DEV, phase_shift.shape[1], phase_shift.shape[2])
    absorb_groups = absorption.reshape(N_DEPTH, SL_DEV, absorption.shape[1], absorption.shape[2])

    def one_slice(field, objects):
        trans = transmission(objects[0], objects[1])
        moved = modulate(field, trans)
        padded = jnp.pad(moved, ((0, 0), (0, 0), (HALF, HALF), (0, 0)))
        rows_done = apply_taps(padded, kernel, 2)
        padded = jnp.pad(rows_done, ((0, 0), (0, 0), (0, 0), (HALF, HALF)))
        return (apply_taps(padded, kernel, 3), None)

    def one_section(field, objects):
        field, unused = lax.scan(one_slice, field, objects)
        return (field, field)
    final, exit_waves = lax.scan(one_section, incident.astype(jnp.float32), (phase_groups, absorb_groups))
    return exit_waves
```

```python
import jax
import jax.numpy as jnp
from jax import lax
from jax.sharding import PartitionSpec as P

TAPS = 33
HALF = 16


def toeplitz(kernel, n_out, n_in, shift):
    outer = jnp.arange(n_out, dtype=jnp.int32)[:, None]
    inner = jnp.arange(n_in, dtype=jnp.int32)[None, :]
    offsets = inner - outer + shift
    onehot = (offsets[:, :, None] == jnp.arange(TAPS, dtype=jnp.int32)[None, None, :]).astype(
        jnp.float32
    )
    band_real = jnp.einsum("abk,k->ab", onehot, kernel[0], precision=lax.Precision.HIGHEST)
    band_imag = jnp.einsum("abk,k->ab", onehot, kernel[1], precision=lax.Precision.HIGHEST)
    top = jnp.stack([band_real, -band_imag], axis=0)
    bottom = jnp.stack([band_imag, band_real], axis=0)
    return jnp.stack([top, bottom], axis=0)


def transmission(phase_part, absorb_part):
    amplitude = jnp.exp(-absorb_part.astype(jnp.float32))
    angle_part = phase_part.astype(jnp.float32)
    return jnp.stack([amplitude * jnp.cos(angle_part), amplitude * jnp.sin(angle_part)], axis=-3)


def modulate(field, trans):
    field_real = field[:, 0]
    field_imag = field[:, 1]
    return jnp.stack(
        [
            field_real * trans[0] - field_imag * trans[1],
            field_real * trans[1] + field_imag * trans[0],
        ],
        axis=1,
    )


def send_packed(pieces, axis, pairs):
    flat = jnp.concatenate([piece.reshape(-1) for piece in pieces])
    moved = lax.ppermute(flat, axis, pairs)
    out, start = [], 0
    for piece in pieces:
        out.append(moved[start:start + piece.size].reshape(piece.shape))
        start += piece.size
    return out


def grow(arrays, row_halos, col_halo):
    tiles = lax.axis_size("tile")
    wave = lax.axis_index("wave")
    down = [(i, i + 1) for i in range(tiles - 1)]
    up = [(i + 1, i) for i in range(tiles - 1)]
    tails = [a[..., a.shape[-2] - r:, :] for a, r in zip(arrays, row_halos)]
    heads = [a[..., :r, :] for a, r in zip(arrays, row_halos)]
    from_prev = send_packed(tails, "tile", down)
    from_next = send_packed(heads, "tile", up)
    tall = [
        jnp.concatenate([p, a, n], axis=-2) for p, a, n in zip(from_prev, arrays, from_next)
    ]
    width = tall[0].shape[-1]
    edges = [
        jnp.where(wave == 0, t[..., width - col_halo:], t[..., :col_halo]) for t in tall
    ]
    got = send_packed(edges, "wave", [(0, 1), (1, 0)])
    out = []
    for t, g in zip(tall, got):
        joined = jnp.concatenate([g, t, g], axis=-1)
        out.append(lax.dynamic_slice_in_dim(joined, col_halo * (1 - wave), width + col_halo, axis=-1))
    return out


def per_device(incident, phase_shift, absorption, fir_taps):
    kernel = fir_taps / jnp.sqrt(jnp.sum(fir_taps * fir_taps) + 1e-06)
    depth_index = lax.axis_index("depth")
    depth_count = lax.axis_size("depth")
    wave = lax.axis_index("wave")
    slices = phase_shift.shape[0]
    rows, cols = incident.shape[2], incident.shape[3]
    reach = HALF * slices
    assert reach <= rows and reach <= cols

    trans_own = transmission(phase_shift, absorption)
    row_halos = [reach - HALF * s for s in range(slices)]
    grown = grow([incident] + [trans_own[s] for s in range(slices)], [reach] + row_halos, reach)
    first_field = grown[0]
    trans_reg = grown[1:]
    width = cols + reach

    col_band = toeplitz(kernel, width, width, HALF)
    row_bands = [
        toeplitz(kernel, rows + 2 * reach - 2 * HALF * (s + 1), rows + 2 * reach - 2 * HALF * s, 0)
        for s in range(slices)
    ]

    def depth_section(field):
        current = field
        for s in range(slices):
            moved = modulate(current, trans_reg[s])
            rows_done = jnp.einsum(
                "dcab,icbj->idaj", row_bands[s], moved, precision=lax.Precision.HIGHEST
            )
            current = jnp.einsum(
                "dcyj,icxj->idxy", col_band, rows_done, precision=lax.Precision.HIGHEST
            )
        return lax.dynamic_slice_in_dim(current, reach * wave, cols, axis=-1)

    exits = jnp.zeros(incident.shape, jnp.float32)
    carried = None
    for step in range(depth_count):
        if step == 0:
            field = first_field
        else:
            field = grow([carried], [reach], reach)[0]
        result = depth_section(field)
        exits = jnp.where(depth_index == step, result, exits)
        if step + 1 < depth_count:
            carried = lax.ppermute(
                result, "depth", [(i, i + 1) for i in range(depth_count - 1)]
            )
    return exits[None]


def solution(mesh):
    return jax.shard_map(
        per_device,
        mesh=mesh,
        in_specs=(
            P(None, None, ("groups", "tile"), "wave"),
            P("depth", ("groups", "tile"), "wave"),
            P("depth", ("groups", "tile"), "wave"),
            P(),
        ),
        out_specs=P("depth", None, None, ("groups", "tile"), "wave"),
        check_vma=False,
    )
```

```python
import jax
import jax.numpy as jnp
from jax import lax
from jax.sharding import PartitionSpec as P

TAPS = 33
HALF = 16


def toeplitz(kernel, size, shift):
    outer = jnp.arange(size, dtype=jnp.int32)[:, None]
    inner = jnp.arange(size, dtype=jnp.int32)[None, :]
    offsets = inner - outer + shift
    band_real = jnp.zeros((size, size), jnp.float32)
    band_imag = jnp.zeros((size, size), jnp.float32)
    for tap in range(TAPS):
        hit = offsets == tap
        band_real = jnp.where(hit, kernel[0, tap], band_real)
        band_imag = jnp.where(hit, kernel[1, tap], band_imag)
    top = jnp.stack([band_real, -band_imag], axis=0)
    bottom = jnp.stack([band_imag, band_real], axis=0)
    return jnp.stack([top, bottom], axis=0)


def transmission(phase_part, absorb_part):
    amplitude = jnp.exp(-absorb_part.astype(jnp.float32))
    angle_part = phase_part.astype(jnp.float32)
    return jnp.stack([amplitude * jnp.cos(angle_part), amplitude * jnp.sin(angle_part)], axis=-3)


def modulate(field, trans):
    field_real = field[:, 0]
    field_imag = field[:, 1]
    return jnp.stack(
        [
            field_real * trans[0] - field_imag * trans[1],
            field_real * trans[1] + field_imag * trans[0],
        ],
        axis=1,
    )


def grow(stack, halo):
    tiles = lax.axis_size("tile")
    wave = lax.axis_index("wave")
    rows = stack.shape[-2]
    from_prev = lax.ppermute(stack[:, rows - halo:], "tile", [(i, i + 1) for i in range(tiles - 1)])
    from_next = lax.ppermute(stack[:, :halo], "tile", [(i + 1, i) for i in range(tiles - 1)])
    tall = jnp.concatenate([from_prev, stack, from_next], axis=-2)
    width = tall.shape[-1]
    edge = jnp.where(wave == 0, tall[..., width - halo:], tall[..., :halo])
    got = lax.ppermute(edge, "wave", [(0, 1), (1, 0)])
    joined = jnp.concatenate([got, tall, got], axis=-1)
    return lax.dynamic_slice_in_dim(joined, halo * (1 - wave), width + halo, axis=-1)


def per_device(incident, phase_shift, absorption, fir_taps):
    kernel = fir_taps / jnp.sqrt(jnp.sum(fir_taps * fir_taps) + 1e-06)
    depth_index = lax.axis_index("depth")
    depth_count = lax.axis_size("depth")
    wave = lax.axis_index("wave")
    slices = phase_shift.shape[0]
    rows, cols = incident.shape[2], incident.shape[3]
    reach = HALF * slices
    assert reach <= rows and reach <= cols

    trans_own = transmission(phase_shift, absorption)
    illum = incident.shape[0]
    grown = grow(
        jnp.concatenate([incident.reshape(2 * illum, rows, cols), trans_own.reshape(2 * slices, rows, cols)]),
        reach,
    )
    first_field = grown[: 2 * illum].reshape(illum, 2, rows + 2 * reach, cols + reach)
    trans_reg = grown[2 * illum:].reshape(slices, 2, rows + 2 * reach, cols + reach)
    width = cols + reach
    tall = rows + 2 * reach

    band = toeplitz(kernel, max(tall, width), HALF)
    col_band = band[:, :, :width, :width]
    row_bands = [
        band[:, :, HALF * (s + 1): tall - HALF * (s + 1), HALF * s: tall - HALF * s]
        for s in range(slices)
    ]

    def depth_section(field):
        current = field
        for s in range(slices):
            moved = modulate(current, trans_reg[s, :, HALF * s: tall - HALF * s])
            rows_done = jnp.einsum(
                "dcab,icbj->idaj", row_bands[s], moved, precision=lax.Precision.HIGHEST
            )
            current = jnp.einsum(
                "dcyj,icxj->idxy", col_band, rows_done, precision=lax.Precision.HIGHEST
            )
        return lax.dynamic_slice_in_dim(current, reach * wave, cols, axis=-1)

    exits = jnp.zeros(incident.shape, jnp.float32)
    carried = None
    for step in range(depth_count):
        if step == 0:
            field = first_field
        else:
            field = grow(carried.reshape(2 * illum, rows, cols), reach).reshape(
                illum, 2, tall, width
            )
        result = depth_section(field)
        exits = jnp.where(depth_index == step, result, exits)
        if step + 1 < depth_count:
            carried = lax.ppermute(
                result, "depth", [(i, i + 1) for i in range(depth_count - 1)]
            )
    return exits[None]


def solution(mesh):
    return jax.shard_map(
        per_device,
        mesh=mesh,
        in_specs=(
            P(None, None, ("groups", "tile"), "wave"),
            P("depth", ("groups", "tile"), "wave"),
            P("depth", ("groups", "tile"), "wave"),
            P(),
        ),
        out_specs=P("depth", None, None, ("groups", "tile"), "wave"),
        check_vma=False,
    )
```

```python
import jax
import jax.numpy as jnp
from jax import lax
from jax.sharding import PartitionSpec as P

TAPS = 33
HALF = 16


def toeplitz(kernel, size, shift):
    period = 2 * size
    gap = jnp.zeros((2, period - TAPS), jnp.float32)
    base = jnp.concatenate([kernel[:, shift:], gap, kernel[:, :shift]], axis=1)
    rolled = jnp.tile(base, (1, size))[:, : size * (period - 1)]
    bands = rolled.reshape(2, size, period - 1)[:, :, :size]
    band_real, band_imag = bands[0], bands[1]
    top = jnp.stack([band_real, -band_imag], axis=0)
    bottom = jnp.stack([band_imag, band_real], axis=0)
    return jnp.stack([top, bottom], axis=0)


def transmission(phase_part, absorb_part):
    amplitude = jnp.exp(-absorb_part.astype(jnp.float32))
    angle_part = phase_part.astype(jnp.float32)
    return jnp.stack([amplitude * jnp.cos(angle_part), amplitude * jnp.sin(angle_part)], axis=-3)


def modulate(field, trans):
    field_real = field[:, 0]
    field_imag = field[:, 1]
    return jnp.stack(
        [
            field_real * trans[0] - field_imag * trans[1],
            field_real * trans[1] + field_imag * trans[0],
        ],
        axis=1,
    )


def grow(stack, halo):
    tiles = lax.axis_size("tile")
    wave = lax.axis_index("wave")
    rows = stack.shape[-2]
    from_prev = lax.ppermute(stack[:, rows - halo:], "tile", [(i, i + 1) for i in range(tiles - 1)])
    from_next = lax.ppermute(stack[:, :halo], "tile", [(i + 1, i) for i in range(tiles - 1)])
    tall = jnp.concatenate([from_prev, stack, from_next], axis=-2)
    width = tall.shape[-1]
    edge = jnp.where(wave == 0, tall[..., width - halo:], tall[..., :halo])
    got = lax.ppermute(edge, "wave", [(0, 1), (1, 0)])
    joined = jnp.concatenate([got, tall, got], axis=-1)
    return lax.dynamic_slice_in_dim(joined, halo * (1 - wave), width + halo, axis=-1)


def per_device(incident, phase_shift, absorption, fir_taps):
    kernel = fir_taps / jnp.sqrt(jnp.sum(fir_taps * fir_taps) + 1e-06)
    depth_index = lax.axis_index("depth")
    depth_count = lax.axis_size("depth")
    wave = lax.axis_index("wave")
    slices = phase_shift.shape[0]
    rows, cols = incident.shape[2], incident.shape[3]
    reach = HALF * slices
    assert reach <= rows and reach <= cols

    trans_own = transmission(phase_shift, absorption)
    illum = incident.shape[0]
    grown = grow(
        jnp.concatenate([incident.reshape(2 * illum, rows, cols), trans_own.reshape(2 * slices, rows, cols)]),
        reach,
    )
    first_field = grown[: 2 * illum].reshape(illum, 2, rows + 2 * reach, cols + reach)
    trans_reg = grown[2 * illum:].reshape(slices, 2, rows + 2 * reach, cols + reach)
    width = cols + reach
    tall = rows + 2 * reach

    band = toeplitz(kernel, max(tall, width), HALF)
    col_band = band[:, :, :width, :width]
    row_bands = [
        band[:, :, HALF * (s + 1): tall - HALF * (s + 1), HALF * s: tall - HALF * s]
        for s in range(slices)
    ]

    def depth_section(field):
        current = field
        for s in range(slices):
            moved = modulate(current, trans_reg[s, :, HALF * s: tall - HALF * s])
            rows_done = jnp.einsum(
                "dcab,icbj->idaj", row_bands[s], moved, precision=lax.Precision.HIGHEST
            )
            current = jnp.einsum(
                "dcyj,icxj->idxy", col_band, rows_done, precision=lax.Precision.HIGHEST
            )
        return lax.dynamic_slice_in_dim(current, reach * wave, cols, axis=-1)

    exits = jnp.zeros(incident.shape, jnp.float32)
    carried = None
    for step in range(depth_count):
        if step == 0:
            field = first_field
        else:
            field = grow(carried.reshape(2 * illum, rows, cols), reach).reshape(
                illum, 2, tall, width
            )
        result = depth_section(field)
        exits = jnp.where(depth_index == step, result, exits)
        if step + 1 < depth_count:
            carried = lax.ppermute(
                result, "depth", [(i, i + 1) for i in range(depth_count - 1)]
            )
    return exits[None]


def solution(mesh):
    return jax.shard_map(
        per_device,
        mesh=mesh,
        in_specs=(
            P(None, None, ("groups", "tile"), "wave"),
            P("depth", ("groups", "tile"), "wave"),
            P("depth", ("groups", "tile"), "wave"),
            P(),
        ),
        out_specs=P("depth", None, None, ("groups", "tile"), "wave"),
        check_vma=False,
    )
```

```python
import jax
import jax.numpy as jnp
from jax import lax
from jax.sharding import PartitionSpec as P

TAPS = 33
HALF = 16


def toeplitz(kernel, size, shift):
    period = 2 * size
    gap = jnp.zeros((2, period - TAPS), jnp.float32)
    base = jnp.concatenate([kernel[:, shift:], gap, kernel[:, :shift]], axis=1)
    rolled = jnp.tile(base, (1, size))[:, : size * (period - 1)]
    bands = rolled.reshape(2, size, period - 1)[:, :, :size]
    band_real, band_imag = bands[0], bands[1]
    top = jnp.stack([band_real, -band_imag], axis=0)
    bottom = jnp.stack([band_imag, band_real], axis=0)
    return jnp.stack([top, bottom], axis=0)


def transmission(phase_part, absorb_part):
    amplitude = jnp.exp(-absorb_part.astype(jnp.float32))
    angle_part = phase_part.astype(jnp.float32)
    return jnp.stack([amplitude * jnp.cos(angle_part), amplitude * jnp.sin(angle_part)], axis=-3)


def modulate(field, trans):
    field_real = field[:, 0]
    field_imag = field[:, 1]
    return jnp.stack(
        [
            field_real * trans[0] - field_imag * trans[1],
            field_real * trans[1] + field_imag * trans[0],
        ],
        axis=1,
    )


def grow(stack, halo):
    tiles = lax.axis_size("tile")
    wave = lax.axis_index("wave")
    rows = stack.shape[-2]
    from_prev = lax.ppermute(stack[:, rows - halo:], "tile", [(i, i + 1) for i in range(tiles - 1)])
    from_next = lax.ppermute(stack[:, :halo], "tile", [(i + 1, i) for i in range(tiles - 1)])
    tall = jnp.concatenate([from_prev, stack, from_next], axis=-2)
    width = tall.shape[-1]
    edge = jnp.where(wave == 0, tall[..., width - halo:], tall[..., :halo])
    got = lax.ppermute(edge, "wave", [(0, 1), (1, 0)])
    joined = jnp.concatenate([got, tall, got], axis=-1)
    return lax.dynamic_slice_in_dim(joined, halo * (1 - wave), width + halo, axis=-1)


def per_device(incident, phase_shift, absorption, fir_taps):
    kernel = fir_taps / jnp.sqrt(jnp.sum(fir_taps * fir_taps) + 1e-06)
    depth_index = lax.axis_index("depth")
    depth_count = lax.axis_size("depth")
    wave = lax.axis_index("wave")
    slices = phase_shift.shape[0]
    rows, cols = incident.shape[2], incident.shape[3]
    reach = HALF * slices
    assert reach <= rows and reach <= cols

    trans_own = transmission(phase_shift, absorption)
    illum = incident.shape[0]
    grown = grow(
        jnp.concatenate([incident.reshape(2 * illum, rows, cols), trans_own.reshape(2 * slices, rows, cols)]),
        reach,
    )
    first_field = grown[: 2 * illum].reshape(illum, 2, rows + 2 * reach, cols + reach)
    trans_reg = grown[2 * illum:].reshape(slices, 2, rows + 2 * reach, cols + reach)
    width = cols + reach
    tall = rows + 2 * reach

    band = toeplitz(kernel, max(tall, width), HALF)
    col_band = band[:, :, :width, :width]
    row_bands = [
        band[:, :, HALF * (s + 1): tall - HALF * (s + 1), HALF * s: tall - HALF * s]
        for s in range(slices)
    ]

    def depth_section(field):
        current = field
        for s in range(slices):
            moved = modulate(current, trans_reg[s, :, HALF * s: tall - HALF * s])
            rows_done = jnp.einsum(
                "dcab,icbj->idaj", row_bands[s], moved, precision=lax.Precision.HIGH
            )
            current = jnp.einsum(
                "dcyj,icxj->idxy", col_band, rows_done, precision=lax.Precision.HIGH
            )
        return lax.dynamic_slice_in_dim(current, reach * wave, cols, axis=-1)

    exits = jnp.zeros(incident.shape, jnp.float32)
    carried = None
    for step in range(depth_count):
        if step == 0:
            field = first_field
        else:
            field = grow(carried.reshape(2 * illum, rows, cols), reach).reshape(
                illum, 2, tall, width
            )
        result = depth_section(field)
        exits = jnp.where(depth_index == step, result, exits)
        if step + 1 < depth_count:
            carried = lax.ppermute(
                result, "depth", [(i, i + 1) for i in range(depth_count - 1)]
            )
    return exits[None]


def solution(mesh):
    return jax.shard_map(
        per_device,
        mesh=mesh,
        in_specs=(
            P(None, None, ("groups", "tile"), "wave"),
            P("depth", ("groups", "tile"), "wave"),
            P("depth", ("groups", "tile"), "wave"),
            P(),
        ),
        out_specs=P("depth", None, None, ("groups", "tile"), "wave"),
        check_vma=False,
    )
```

```python
import jax
import jax.numpy as jnp
from jax import lax
from jax.sharding import PartitionSpec as P

TAPS = 33
HALF = 16


def toeplitz(kernel, size, shift):
    period = 2 * size
    gap = jnp.zeros((2, period - TAPS), jnp.float32)
    base = jnp.concatenate([kernel[:, shift:], gap, kernel[:, :shift]], axis=1)
    rolled = jnp.tile(base, (1, size))[:, : size * (period - 1)]
    bands = rolled.reshape(2, size, period - 1)[:, :, :size]
    band_real, band_imag = bands[0], bands[1]
    top = jnp.stack([band_real, -band_imag], axis=0)
    bottom = jnp.stack([band_imag, band_real], axis=0)
    return jnp.stack([top, bottom], axis=0)


def transmission(phase_part, absorb_part):
    amplitude = jnp.exp(-absorb_part.astype(jnp.float32))
    angle_part = phase_part.astype(jnp.float32)
    return jnp.stack([amplitude * jnp.cos(angle_part), amplitude * jnp.sin(angle_part)], axis=-3)


def modulate(field, trans):
    field_real = field[:, 0]
    field_imag = field[:, 1]
    return jnp.stack(
        [
            field_real * trans[0] - field_imag * trans[1],
            field_real * trans[1] + field_imag * trans[0],
        ],
        axis=1,
    )


def grow(stack, halo, splits):
    tiles = lax.axis_size("tile")
    wave = lax.axis_index("wave")
    rows, cols = stack.shape[-2], stack.shape[-1]
    from_prev = lax.ppermute(stack[:, rows - halo:], "tile", [(i, i + 1) for i in range(tiles - 1)])
    from_next = lax.ppermute(stack[:, :halo], "tile", [(i + 1, i) for i in range(tiles - 1)])
    tall = jnp.concatenate([from_prev, stack, from_next], axis=-2)
    got = lax.ppermute(tall, "wave", [(0, 1), (1, 0)])
    out, start = [], 0
    for size in splits:
        own, other = tall[start:start + size], got[start:start + size]
        start += size
        left = jnp.concatenate([own, other[..., :halo]], axis=-1)
        right = jnp.concatenate([other[..., cols - halo:], own], axis=-1)
        out.append(jnp.where(wave == 0, left, right))
    return out


def per_device(incident, phase_shift, absorption, fir_taps):
    kernel = fir_taps / jnp.sqrt(jnp.sum(fir_taps * fir_taps) + 1e-06)
    depth_index = lax.axis_index("depth")
    depth_count = lax.axis_size("depth")
    wave = lax.axis_index("wave")
    slices = phase_shift.shape[0]
    rows, cols = incident.shape[2], incident.shape[3]
    reach = HALF * slices
    assert reach <= rows and reach <= cols

    trans_own = transmission(phase_shift, absorption)
    illum = incident.shape[0]
    field_grown, trans_grown = grow(
        jnp.concatenate([incident.reshape(2 * illum, rows, cols), trans_own.reshape(2 * slices, rows, cols)]),
        reach,
        (2 * illum, 2 * slices),
    )
    first_field = field_grown.reshape(illum, 2, rows + 2 * reach, cols + reach)
    trans_reg = trans_grown.reshape(slices, 2, rows + 2 * reach, cols + reach)
    width = cols + reach
    tall = rows + 2 * reach

    band = toeplitz(kernel, max(tall, width), HALF)
    col_band = band[:, :, :width, :width]
    row_bands = [
        band[:, :, HALF * (s + 1): tall - HALF * (s + 1), HALF * s: tall - HALF * s]
        for s in range(slices)
    ]

    def depth_section(field):
        current = field
        for s in range(slices):
            moved = modulate(current, trans_reg[s, :, HALF * s: tall - HALF * s])
            rows_done = jnp.einsum(
                "dcab,icbj->idaj", row_bands[s], moved, precision=lax.Precision.HIGH
            )
            current = jnp.einsum(
                "dcyj,icxj->idxy", col_band, rows_done, precision=lax.Precision.HIGH
            )
        return lax.dynamic_slice_in_dim(current, reach * wave, cols, axis=-1)

    exits = jnp.zeros(incident.shape, jnp.float32)
    carried = None
    for step in range(depth_count):
        if step == 0:
            field = first_field
        else:
            field = grow(carried.reshape(2 * illum, rows, cols), reach, (2 * illum,))[0].reshape(
                illum, 2, tall, width
            )
        result = depth_section(field)
        exits = jnp.where(depth_index == step, result, exits)
        if step + 1 < depth_count:
            carried = lax.ppermute(
                result, "depth", [(i, i + 1) for i in range(depth_count - 1)]
            )
    return exits[None]


def solution(mesh):
    return jax.shard_map(
        per_device,
        mesh=mesh,
        in_specs=(
            P(None, None, ("groups", "tile"), "wave"),
            P("depth", ("groups", "tile"), "wave"),
            P("depth", ("groups", "tile"), "wave"),
            P(),
        ),
        out_specs=P("depth", None, None, ("groups", "tile"), "wave"),
        check_vma=False,
    )
```

```python
import jax
import jax.numpy as jnp
from jax import lax
from jax.sharding import PartitionSpec as P

TAPS = 33
HALF = 16


def toeplitz(kernel, size, shift):
    period = 2 * size
    gap = jnp.zeros((2, period - TAPS), jnp.float32)
    base = jnp.concatenate([kernel[:, shift:], gap, kernel[:, :shift]], axis=1)
    rolled = jnp.tile(base, (1, size))[:, : size * (period - 1)]
    bands = rolled.reshape(2, size, period - 1)[:, :, :size]
    band_real, band_imag = bands[0], bands[1]
    top = jnp.stack([band_real, -band_imag], axis=0)
    bottom = jnp.stack([band_imag, band_real], axis=0)
    return jnp.stack([top, bottom], axis=0)


def transmission(phase_part, absorb_part):
    amplitude = jnp.exp(-absorb_part.astype(jnp.float32))
    angle_part = phase_part.astype(jnp.float32)
    return jnp.stack([amplitude * jnp.cos(angle_part), amplitude * jnp.sin(angle_part)], axis=-3)


def modulate(field, trans):
    field_real = field[:, 0]
    field_imag = field[:, 1]
    return jnp.stack(
        [
            field_real * trans[0] - field_imag * trans[1],
            field_real * trans[1] + field_imag * trans[0],
        ],
        axis=1,
    )


def send_rows(pieces, axis, pairs):
    flat = jnp.concatenate([p.reshape(-1, p.shape[-1]) for p in pieces], axis=0)
    moved = lax.ppermute(flat, axis, pairs)
    out, start = [], 0
    for p in pieces:
        count = p.shape[0] * p.shape[1]
        out.append(moved[start:start + count].reshape(p.shape))
        start += count
    return out


def grow(pieces, row_halos, col_halo):
    tiles = lax.axis_size("tile")
    wave = lax.axis_index("wave")
    cols = pieces[0].shape[-1]
    tails = [p[:, p.shape[1] - r:] for p, r in zip(pieces, row_halos)]
    heads = [p[:, :r] for p, r in zip(pieces, row_halos)]
    from_prev = send_rows(tails, "tile", [(i, i + 1) for i in range(tiles - 1)])
    from_next = send_rows(heads, "tile", [(i + 1, i) for i in range(tiles - 1)])
    talls = [jnp.concatenate(trio, axis=1) for trio in zip(from_prev, pieces, from_next)]
    others = send_rows(talls, "wave", [(0, 1), (1, 0)])
    out = []
    for own, other in zip(talls, others):
        left = jnp.concatenate([own, other[..., :col_halo]], axis=-1)
        right = jnp.concatenate([other[..., cols - col_halo:], own], axis=-1)
        out.append(jnp.where(wave == 0, left, right))
    return out


def per_device(incident, phase_shift, absorption, fir_taps):
    kernel = fir_taps / jnp.sqrt(jnp.sum(fir_taps * fir_taps) + 1e-06)
    depth_index = lax.axis_index("depth")
    depth_count = lax.axis_size("depth")
    wave = lax.axis_index("wave")
    slices = phase_shift.shape[0]
    rows, cols = incident.shape[2], incident.shape[3]
    reach = HALF * slices
    assert reach <= rows and reach <= cols

    trans_own = transmission(phase_shift, absorption)
    illum = incident.shape[0]
    grown = grow(
        [incident.reshape(2 * illum, rows, cols)] + [trans_own[s] for s in range(slices)],
        [reach] + [reach - HALF * s for s in range(slices)],
        reach,
    )
    first_field = grown[0].reshape(illum, 2, rows + 2 * reach, cols + reach)
    trans_reg = grown[1:]
    width = cols + reach
    tall = rows + 2 * reach

    band = toeplitz(kernel, max(tall, width), HALF)
    col_band = band[:, :, :width, :width]
    row_bands = [
        band[:, :, HALF * (s + 1): tall - HALF * (s + 1), HALF * s: tall - HALF * s]
        for s in range(slices)
    ]

    def depth_section(field):
        current = field
        for s in range(slices):
            moved = modulate(current, trans_reg[s])
            rows_done = jnp.einsum(
                "dcab,icbj->idaj", row_bands[s], moved, precision=lax.Precision.HIGH
            )
            current = jnp.einsum(
                "dcyj,icxj->idxy", col_band, rows_done, precision=lax.Precision.HIGH
            )
        return lax.dynamic_slice_in_dim(current, reach * wave, cols, axis=-1)

    exits = jnp.zeros(incident.shape, jnp.float32)
    carried = None
    for step in range(depth_count):
        if step == 0:
            field = first_field
        else:
            field = grow([carried.reshape(2 * illum, rows, cols)], [reach], reach)[0].reshape(
                illum, 2, tall, width
            )
        result = depth_section(field)
        exits = jnp.where(depth_index == step, result, exits)
        if step + 1 < depth_count:
            carried = lax.ppermute(
                result, "depth", [(i, i + 1) for i in range(depth_count - 1)]
            )
    return exits[None]


def solution(mesh):
    return jax.shard_map(
        per_device,
        mesh=mesh,
        in_specs=(
            P(None, None, ("groups", "tile"), "wave"),
            P("depth", ("groups", "tile"), "wave"),
            P("depth", ("groups", "tile"), "wave"),
            P(),
        ),
        out_specs=P("depth", None, None, ("groups", "tile"), "wave"),
        check_vma=False,
    )
```

```python
import jax
import jax.numpy as jnp
from jax import lax
from jax.sharding import PartitionSpec as P

TAPS = 33
HALF = 16


def toeplitz(kernel, size, shift):
    period = 2 * size
    gap = jnp.zeros((2, period - TAPS), jnp.float32)
    base = jnp.concatenate([kernel[:, shift:], gap, kernel[:, :shift]], axis=1)
    rolled = jnp.tile(base, (1, size))[:, : size * (period - 1)]
    bands = rolled.reshape(2, size, period - 1)[:, :, :size]
    band_real, band_imag = bands[0], bands[1]
    top = jnp.stack([band_real, -band_imag], axis=0)
    bottom = jnp.stack([band_imag, band_real], axis=0)
    return jnp.stack([top, bottom], axis=0)


def transmission(phase_part, absorb_part):
    amplitude = jnp.exp(-absorb_part.astype(jnp.float32))
    angle_part = phase_part.astype(jnp.float32)
    return jnp.stack([amplitude * jnp.cos(angle_part), amplitude * jnp.sin(angle_part)], axis=-3)


def modulate(field, trans):
    field_real = field[:, 0]
    field_imag = field[:, 1]
    return jnp.stack(
        [
            field_real * trans[0] - field_imag * trans[1],
            field_real * trans[1] + field_imag * trans[0],
        ],
        axis=1,
    )


def grow(stack, halo, splits):
    tiles = lax.axis_size("tile")
    wave = lax.axis_index("wave")
    rows, cols = stack.shape[-2], stack.shape[-1]
    from_prev = lax.ppermute(stack[:, rows - halo:], "tile", [(i, i + 1) for i in range(tiles - 1)])
    from_next = lax.ppermute(stack[:, :halo], "tile", [(i + 1, i) for i in range(tiles - 1)])
    tall = jnp.concatenate([from_prev, stack, from_next], axis=-2)
    return widen(tall, halo, splits)


def widen(tall, halo, splits):
    wave = lax.axis_index("wave")
    cols = tall.shape[-1]
    got = lax.ppermute(tall, "wave", [(0, 1), (1, 0)])
    out, start = [], 0
    for size in splits:
        own, other = tall[start:start + size], got[start:start + size]
        start += size
        left = jnp.concatenate([own, other[..., :halo]], axis=-1)
        right = jnp.concatenate([other[..., cols - halo:], own], axis=-1)
        out.append(jnp.where(wave == 0, left, right))
    return out


def per_device(incident, phase_shift, absorption, fir_taps):
    kernel = fir_taps / jnp.sqrt(jnp.sum(fir_taps * fir_taps) + 1e-06)
    depth_index = lax.axis_index("depth")
    depth_count = lax.axis_size("depth")
    wave = lax.axis_index("wave")
    slices = phase_shift.shape[0]
    rows, cols = incident.shape[2], incident.shape[3]
    reach = HALF * slices
    assert reach <= rows and reach <= cols

    trans_own = transmission(phase_shift, absorption)
    illum = incident.shape[0]
    field_grown, trans_grown = grow(
        jnp.concatenate([incident.reshape(2 * illum, rows, cols), trans_own.reshape(2 * slices, rows, cols)]),
        reach,
        (2 * illum, 2 * slices),
    )
    first_field = field_grown.reshape(illum, 2, rows + 2 * reach, cols + reach)
    trans_reg = trans_grown.reshape(slices, 2, rows + 2 * reach, cols + reach)
    width = cols + reach
    tall = rows + 2 * reach

    band = toeplitz(kernel, max(tall, width), HALF)
    col_band = band[:, :, :width, :width]
    row_bands = [
        band[:, :, HALF * (s + 1): tall - HALF * (s + 1), HALF * s: tall - HALF * s]
        for s in range(slices)
    ]

    def depth_section(field):
        current = field
        for s in range(slices):
            moved = modulate(current, trans_reg[s, :, HALF * s: tall - HALF * s])
            rows_done = jnp.einsum(
                "dcab,icbj->idaj", row_bands[s], moved, precision=lax.Precision.HIGH
            )
            current = jnp.einsum(
                "dcyj,icxj->idxy", col_band, rows_done, precision=lax.Precision.HIGH
            )
        return lax.dynamic_slice_in_dim(current, reach * wave, cols, axis=-1)

    exits = jnp.zeros(incident.shape, jnp.float32)
    tiles = lax.axis_size("tile")
    spot = lambda t, d: t * depth_count + d
    ahead = range(depth_count - 1)
    own_pairs = [(spot(t, d), spot(t, d + 1)) for t in range(tiles) for d in ahead]
    prev_pairs = [(spot(t - 1, d), spot(t, d + 1)) for t in range(1, tiles) for d in ahead]
    next_pairs = [(spot(t + 1, d), spot(t, d + 1)) for t in range(tiles - 1) for d in ahead]
    field = first_field
    for step in range(depth_count):
        result = depth_section(field)
        exits = jnp.where(depth_index == step, result, exits)
        if step + 1 < depth_count:
            flat = result.reshape(2 * illum, rows, cols)
            grid = ("tile", "depth")
            from_prev = lax.ppermute(flat[:, rows - reach:], grid, prev_pairs)
            mine = lax.ppermute(flat, grid, own_pairs)
            from_next = lax.ppermute(flat[:, :reach], grid, next_pairs)
            field = widen(jnp.concatenate([from_prev, mine, from_next], axis=1), reach, (2 * illum,))[0].reshape(
                illum, 2, tall, width
            )
    return exits[None]


def solution(mesh):
    return jax.shard_map(
        per_device,
        mesh=mesh,
        in_specs=(
            P(None, None, ("groups", "tile"), "wave"),
            P("depth", ("groups", "tile"), "wave"),
            P("depth", ("groups", "tile"), "wave"),
            P(),
        ),
        out_specs=P("depth", None, None, ("groups", "tile"), "wave"),
        check_vma=False,
    )
```

```python
import jax
import jax.numpy as jnp
from jax import lax
from jax.sharding import PartitionSpec as P

TAPS = 33
HALF = 16


def toeplitz(kernel, size, shift):
    period = 2 * size
    gap = jnp.zeros((2, period - TAPS), jnp.float32)
    base = jnp.concatenate([kernel[:, shift:], gap, kernel[:, :shift]], axis=1)
    rolled = jnp.tile(base, (1, size))[:, : size * (period - 1)]
    bands = rolled.reshape(2, size, period - 1)[:, :, :size]
    band_real, band_imag = bands[0], bands[1]
    top = jnp.stack([band_real, -band_imag], axis=0)
    bottom = jnp.stack([band_imag, band_real], axis=0)
    return jnp.stack([top, bottom], axis=0)


def transmission(phase_part, absorb_part):
    amplitude = jnp.exp(-absorb_part.astype(jnp.float32))
    angle_part = phase_part.astype(jnp.float32)
    return jnp.stack([amplitude * jnp.cos(angle_part), amplitude * jnp.sin(angle_part)], axis=-3)


def modulate(field, trans):
    field_real = field[:, 0]
    field_imag = field[:, 1]
    return jnp.stack(
        [
            field_real * trans[0] - field_imag * trans[1],
            field_real * trans[1] + field_imag * trans[0],
        ],
        axis=1,
    )


def grow(stack, halo, splits):
    tiles = lax.axis_size("tile")
    wave = lax.axis_index("wave")
    rows, cols = stack.shape[-2], stack.shape[-1]
    from_prev = lax.ppermute(stack[:, rows - halo:], "tile", [(i, i + 1) for i in range(tiles - 1)])
    from_next = lax.ppermute(stack[:, :halo], "tile", [(i + 1, i) for i in range(tiles - 1)])
    tall = jnp.concatenate([from_prev, stack, from_next], axis=-2)
    return widen(tall, halo, splits)


def widen(tall, halo, splits):
    wave = lax.axis_index("wave")
    cols = tall.shape[-1]
    got = lax.ppermute(tall, "wave", [(0, 1), (1, 0)])
    out, start = [], 0
    for size in splits:
        own, other = tall[start:start + size], got[start:start + size]
        start += size
        left = jnp.concatenate([own, other[..., :halo]], axis=-1)
        right = jnp.concatenate([other[..., cols - halo:], own], axis=-1)
        out.append(jnp.where(wave == 0, left, right))
    return out


def per_device(incident, phase_shift, absorption, fir_taps):
    kernel = fir_taps / jnp.sqrt(jnp.sum(fir_taps * fir_taps) + 1e-06)
    depth_index = lax.axis_index("depth")
    depth_count = lax.axis_size("depth")
    wave = lax.axis_index("wave")
    slices = phase_shift.shape[0]
    rows, cols = incident.shape[2], incident.shape[3]
    reach = HALF * slices
    assert reach <= rows and reach <= cols

    trans_own = transmission(phase_shift, absorption)
    illum = incident.shape[0]
    first_field, trans_head = grow(
        jnp.concatenate([incident.reshape(2 * illum, rows, cols), trans_own[0]]),
        reach,
        (2 * illum, 2),
    )
    (trans_rest,) = grow(trans_own[1:].reshape(2 * slices - 2, rows, cols), reach, (2 * slices - 2,))
    first_field = first_field.reshape(illum, 2, rows + 2 * reach, cols + reach)
    trans_reg = jnp.concatenate([trans_head[None], trans_rest.reshape(slices - 1, 2, rows + 2 * reach, cols + reach)])
    width = cols + reach
    tall = rows + 2 * reach

    band = toeplitz(kernel, max(tall, width), HALF)
    col_band = band[:, :, :width, :width]
    row_bands = [
        band[:, :, HALF * (s + 1): tall - HALF * (s + 1), HALF * s: tall - HALF * s]
        for s in range(slices)
    ]

    def depth_section(field):
        current = field
        for s in range(slices):
            moved = modulate(current, trans_reg[s, :, HALF * s: tall - HALF * s])
            rows_done = jnp.einsum(
                "dcab,icbj->idaj", row_bands[s], moved, precision=lax.Precision.HIGH
            )
            current = jnp.einsum(
                "dcyj,icxj->idxy", col_band, rows_done, precision=lax.Precision.HIGH
            )
        return lax.dynamic_slice_in_dim(current, reach * wave, cols, axis=-1)

    exits = jnp.zeros(incident.shape, jnp.float32)
    tiles = lax.axis_size("tile")
    spot = lambda t, d: t * depth_count + d
    ahead = range(depth_count - 1)
    own_pairs = [(spot(t, d), spot(t, d + 1)) for t in range(tiles) for d in ahead]
    prev_pairs = [(spot(t - 1, d), spot(t, d + 1)) for t in range(1, tiles) for d in ahead]
    next_pairs = [(spot(t + 1, d), spot(t, d + 1)) for t in range(tiles - 1) for d in ahead]
    field = first_field
    for step in range(depth_count):
        result = depth_section(field)
        exits = jnp.where(depth_index == step, result, exits)
        if step + 1 < depth_count:
            flat = result.reshape(2 * illum, rows, cols)
            grid = ("tile", "depth")
            from_prev = lax.ppermute(flat[:, rows - reach:], grid, prev_pairs)
            mine = lax.ppermute(flat, grid, own_pairs)
            from_next = lax.ppermute(flat[:, :reach], grid, next_pairs)
            field = widen(jnp.concatenate([from_prev, mine, from_next], axis=1), reach, (2 * illum,))[0].reshape(
                illum, 2, tall, width
            )
    return exits[None]


def solution(mesh):
    return jax.shard_map(
        per_device,
        mesh=mesh,
        in_specs=(
            P(None, None, ("groups", "tile"), "wave"),
            P("depth", ("groups", "tile"), "wave"),
            P("depth", ("groups", "tile"), "wave"),
            P(),
        ),
        out_specs=P("depth", None, None, ("groups", "tile"), "wave"),
        check_vma=False,
    )
```

```python
import jax
import jax.numpy as jnp
from jax import lax
from jax.sharding import PartitionSpec as P

TAPS = 33
HALF = 16


def toeplitz(kernel, size, shift):
    period = 2 * size
    gap = jnp.zeros((2, period - TAPS), jnp.float32)
    base = jnp.concatenate([kernel[:, shift:], gap, kernel[:, :shift]], axis=1)
    rolled = jnp.tile(base, (1, size))[:, : size * (period - 1)]
    bands = rolled.reshape(2, size, period - 1)[:, :, :size]
    band_real, band_imag = bands[0], bands[1]
    top = jnp.stack([band_real, -band_imag], axis=0)
    bottom = jnp.stack([band_imag, band_real], axis=0)
    return jnp.stack([top, bottom], axis=0)


def transmission(phase_part, absorb_part):
    amplitude = jnp.exp(-absorb_part.astype(jnp.float32))
    angle_part = phase_part.astype(jnp.float32)
    return jnp.stack([amplitude * jnp.cos(angle_part), amplitude * jnp.sin(angle_part)], axis=-3)


def modulate(field, trans):
    field_real = field[:, 0]
    field_imag = field[:, 1]
    return jnp.stack(
        [
            field_real * trans[0] - field_imag * trans[1],
            field_real * trans[1] + field_imag * trans[0],
        ],
        axis=1,
    )


def grow(stack, halo, splits, rider):
    tiles = lax.axis_size("tile")
    wave = lax.axis_index("wave")
    rows, cols = stack.shape[-2], stack.shape[-1]
    from_prev = lax.ppermute(stack[:, rows - halo:], "tile", [(i, i + 1) for i in range(tiles - 1)])
    from_next = lax.ppermute(stack[:, :halo], "tile", [(i + 1, i) for i in range(tiles - 1)])
    tall = jnp.concatenate([from_prev, stack, from_next], axis=-2)
    rider, tall = lax.optimization_barrier((rider, tall))
    return widen(tall, halo, splits), rider


def widen(tall, halo, splits):
    wave = lax.axis_index("wave")
    cols = tall.shape[-1]
    got = lax.ppermute(tall, "wave", [(0, 1), (1, 0)])
    out, start = [], 0
    for size in splits:
        own, other = tall[start:start + size], got[start:start + size]
        start += size
        left = jnp.concatenate([own, other[..., :halo]], axis=-1)
        right = jnp.concatenate([other[..., cols - halo:], own], axis=-1)
        out.append(jnp.where(wave == 0, left, right))
    return out


def per_device(incident, phase_shift, absorption, fir_taps):
    kernel = fir_taps / jnp.sqrt(jnp.sum(fir_taps * fir_taps) + 1e-06)
    depth_index = lax.axis_index("depth")
    depth_count = lax.axis_size("depth")
    wave = lax.axis_index("wave")
    slices = phase_shift.shape[0]
    rows, cols = incident.shape[2], incident.shape[3]
    reach = HALF * slices
    assert reach <= rows and reach <= cols

    trans_own = transmission(phase_shift, absorption)
    illum = incident.shape[0]
    width = cols + reach
    tall = rows + 2 * reach
    band = toeplitz(kernel, max(tall, width), HALF)
    (field_grown, trans_grown), band = grow(
        jnp.concatenate([incident.reshape(2 * illum, rows, cols), trans_own.reshape(2 * slices, rows, cols)]),
        reach,
        (2 * illum, 2 * slices),
        band,
    )
    first_field = field_grown.reshape(illum, 2, rows + 2 * reach, cols + reach)
    trans_reg = trans_grown.reshape(slices, 2, rows + 2 * reach, cols + reach)
    col_band = band[:, :, :width, :width]
    row_bands = [
        band[:, :, HALF * (s + 1): tall - HALF * (s + 1), HALF * s: tall - HALF * s]
        for s in range(slices)
    ]

    def depth_section(field):
        current = field
        for s in range(slices):
            moved = modulate(current, trans_reg[s, :, HALF * s: tall - HALF * s])
            rows_done = jnp.einsum(
                "dcab,icbj->idaj", row_bands[s], moved, precision=lax.Precision.HIGH
            )
            current = jnp.einsum(
                "dcyj,icxj->idxy", col_band, rows_done, precision=lax.Precision.HIGH
            )
        return lax.dynamic_slice_in_dim(current, reach * wave, cols, axis=-1)

    exits = jnp.zeros(incident.shape, jnp.float32)
    tiles = lax.axis_size("tile")
    spot = lambda t, d: t * depth_count + d
    ahead = range(depth_count - 1)
    own_pairs = [(spot(t, d), spot(t, d + 1)) for t in range(tiles) for d in ahead]
    prev_pairs = [(spot(t - 1, d), spot(t, d + 1)) for t in range(1, tiles) for d in ahead]
    next_pairs = [(spot(t + 1, d), spot(t, d + 1)) for t in range(tiles - 1) for d in ahead]
    field = first_field
    for step in range(depth_count):
        result = depth_section(field)
        exits = jnp.where(depth_index == step, result, exits)
        if step + 1 < depth_count:
            flat = result.reshape(2 * illum, rows, cols)
            grid = ("tile", "depth")
            from_prev = lax.ppermute(flat[:, rows - reach:], grid, prev_pairs)
            mine = lax.ppermute(flat, grid, own_pairs)
            from_next = lax.ppermute(flat[:, :reach], grid, next_pairs)
            field = widen(jnp.concatenate([from_prev, mine, from_next], axis=1), reach, (2 * illum,))[0].reshape(
                illum, 2, tall, width
            )
    return exits[None]


def solution(mesh):
    return jax.shard_map(
        per_device,
        mesh=mesh,
        in_specs=(
            P(None, None, ("groups", "tile"), "wave"),
            P("depth", ("groups", "tile"), "wave"),
            P("depth", ("groups", "tile"), "wave"),
            P(),
        ),
        out_specs=P("depth", None, None, ("groups", "tile"), "wave"),
        check_vma=False,
    )
```

```python
import jax
import jax.numpy as jnp
from jax import lax
from jax.sharding import PartitionSpec as P

TAPS = 33
HALF = 16


def toeplitz(kernel, size, shift):
    period = 2 * size
    gap = jnp.zeros((2, period - TAPS), jnp.float32)
    base = jnp.concatenate([kernel[:, shift:], gap, kernel[:, :shift]], axis=1)
    rolled = jnp.tile(base, (1, size))[:, : size * (period - 1)]
    bands = rolled.reshape(2, size, period - 1)[:, :, :size]
    band_real, band_imag = bands[0], bands[1]
    top = jnp.stack([band_real, -band_imag], axis=0)
    bottom = jnp.stack([band_imag, band_real], axis=0)
    return jnp.stack([top, bottom], axis=0)


def transmission(phase_part, absorb_part):
    amplitude = jnp.exp(-absorb_part.astype(jnp.float32))
    angle_part = phase_part.astype(jnp.float32)
    return jnp.stack([amplitude * jnp.cos(angle_part), amplitude * jnp.sin(angle_part)], axis=-3)


def modulate(field, trans):
    field_real = field[:, 0]
    field_imag = field[:, 1]
    return jnp.stack(
        [
            field_real * trans[0] - field_imag * trans[1],
            field_real * trans[1] + field_imag * trans[0],
        ],
        axis=1,
    )


def grow(stack, halo, splits, rider):
    tiles = lax.axis_size("tile")
    wave = lax.axis_index("wave")
    rows, cols = stack.shape[-2], stack.shape[-1]
    from_prev = lax.ppermute(stack[:, rows - halo:], "tile", [(i, i + 1) for i in range(tiles - 1)])
    from_next = lax.ppermute(stack[:, :halo], "tile", [(i + 1, i) for i in range(tiles - 1)])
    tall = jnp.concatenate([from_prev, stack, from_next], axis=-2)
    rider, tall = lax.optimization_barrier((rider, tall))
    return widen(tall, halo, splits), rider


def widen(tall, halo, splits):
    wave = lax.axis_index("wave")
    cols = tall.shape[-1]
    got = lax.ppermute(tall, "wave", [(0, 1), (1, 0)])
    out, start = [], 0
    for size in splits:
        own, other = tall[start:start + size], got[start:start + size]
        start += size
        left = jnp.concatenate([own, other[..., :halo]], axis=-1)
        right = jnp.concatenate([other[..., cols - halo:], own], axis=-1)
        out.append(jnp.where(wave == 0, left, right))
    return out


def per_device(incident, phase_shift, absorption, fir_taps):
    kernel = fir_taps / jnp.sqrt(jnp.sum(fir_taps * fir_taps) + 1e-06)
    depth_index = lax.axis_index("depth")
    depth_count = lax.axis_size("depth")
    wave = lax.axis_index("wave")
    slices = phase_shift.shape[0]
    rows, cols = incident.shape[2], incident.shape[3]
    reach = HALF * slices
    assert reach <= rows and reach <= cols

    trans_own = transmission(phase_shift, absorption)
    illum = incident.shape[0]
    width = cols + reach
    tall = rows + 2 * reach
    band = toeplitz(kernel, max(tall, width), HALF)
    (field_grown, trans_grown), band = grow(
        jnp.concatenate([incident.reshape(2 * illum, rows, cols), trans_own.reshape(2 * slices, rows, cols)]),
        reach,
        (2 * illum, 2 * slices),
        band,
    )
    first_field = field_grown.reshape(illum, 2, rows + 2 * reach, cols + reach)
    trans_reg = trans_grown.reshape(slices, 2, rows + 2 * reach, cols + reach)
    col_band = band[:, :, :width, :width]
    row_bands = [
        band[:, :, HALF * (s + 1): tall - HALF * (s + 1), HALF * s: tall - HALF * s]
        for s in range(slices)
    ]

    last_band = jnp.where(wave == 0, col_band[:, :, :cols], col_band[:, :, reach:reach + cols])

    def depth_section(field):
        current = field
        for s in range(slices):
            moved = modulate(current, trans_reg[s, :, HALF * s: tall - HALF * s])
            rows_done = jnp.einsum(
                "dcab,icbj->idaj", row_bands[s], moved, precision=lax.Precision.HIGH
            )
            current = jnp.einsum(
                "dcyj,icxj->idxy",
                last_band if s == slices - 1 else col_band,
                rows_done,
                precision=lax.Precision.HIGH,
            )
        return current

    exits = jnp.zeros(incident.shape, jnp.float32)
    tiles = lax.axis_size("tile")
    spot = lambda t, d: t * depth_count + d
    ahead = range(depth_count - 1)
    own_pairs = [(spot(t, d), spot(t, d + 1)) for t in range(tiles) for d in ahead]
    prev_pairs = [(spot(t - 1, d), spot(t, d + 1)) for t in range(1, tiles) for d in ahead]
    next_pairs = [(spot(t + 1, d), spot(t, d + 1)) for t in range(tiles - 1) for d in ahead]
    field = first_field
    for step in range(depth_count):
        result = depth_section(field)
        exits = jnp.where(depth_index == step, result, exits)
        if step + 1 < depth_count:
            flat = result.reshape(2 * illum, rows, cols)
            grid = ("tile", "depth")
            from_prev = lax.ppermute(flat[:, rows - reach:], grid, prev_pairs)
            mine = lax.ppermute(flat, grid, own_pairs)
            from_next = lax.ppermute(flat[:, :reach], grid, next_pairs)
            field = widen(jnp.concatenate([from_prev, mine, from_next], axis=1), reach, (2 * illum,))[0].reshape(
                illum, 2, tall, width
            )
    return exits[None]


def solution(mesh):
    return jax.shard_map(
        per_device,
        mesh=mesh,
        in_specs=(
            P(None, None, ("groups", "tile"), "wave"),
            P("depth", ("groups", "tile"), "wave"),
            P("depth", ("groups", "tile"), "wave"),
            P(),
        ),
        out_specs=P("depth", None, None, ("groups", "tile"), "wave"),
        check_vma=False,
    )
```

```python
import jax
import jax.numpy as jnp
from jax import lax
from jax.sharding import PartitionSpec as P

TAPS = 33
HALF = 16


def toeplitz(kernel, size, shift):
    period = 2 * size
    gap = jnp.zeros((2, period - TAPS), jnp.float32)
    base = jnp.concatenate([kernel[:, shift:], gap, kernel[:, :shift]], axis=1)
    rolled = jnp.tile(base, (1, size))[:, : size * (period - 1)]
    bands = rolled.reshape(2, size, period - 1)[:, :, :size]
    band_real, band_imag = bands[0], bands[1]
    top = jnp.stack([band_real, -band_imag], axis=0)
    bottom = jnp.stack([band_imag, band_real], axis=0)
    return jnp.stack([top, bottom], axis=0)


def transmission(phase_part, absorb_part):
    amplitude = jnp.exp(-absorb_part.astype(jnp.float32))
    angle_part = phase_part.astype(jnp.float32)
    return jnp.stack([amplitude * jnp.cos(angle_part), amplitude * jnp.sin(angle_part)], axis=-3)


def modulate(field, trans):
    field_real = field[:, 0]
    field_imag = field[:, 1]
    return jnp.stack(
        [
            field_real * trans[0] - field_imag * trans[1],
            field_real * trans[1] + field_imag * trans[0],
        ],
        axis=1,
    )


def grow(stack, halo, splits, rider):
    tiles = lax.axis_size("tile")
    wave = lax.axis_index("wave")
    rows, cols = stack.shape[-2], stack.shape[-1]
    from_prev = lax.ppermute(stack[:, rows - halo:], "tile", [(i, i + 1) for i in range(tiles - 1)])
    from_next = lax.ppermute(stack[:, :halo], "tile", [(i + 1, i) for i in range(tiles - 1)])
    tall = jnp.concatenate([from_prev, stack, from_next], axis=-2)
    rider, tall = lax.optimization_barrier((rider, tall))
    return widen(tall, halo, splits), rider


def widen(tall, halo, splits):
    wave = lax.axis_index("wave")
    cols = tall.shape[-1]
    got = lax.ppermute(tall, "wave", [(0, 1), (1, 0)])
    out, start = [], 0
    for size in splits:
        own, other = tall[start:start + size], got[start:start + size]
        start += size
        part = jnp.where(wave == 0, other[..., :halo], jnp.flip(other[..., cols - halo:], axis=-1))
        out.append(jnp.concatenate([own, part], axis=-1))
    return out


def per_device(incident, phase_shift, absorption, fir_taps):
    kernel = fir_taps / jnp.sqrt(jnp.sum(fir_taps * fir_taps) + 1e-06)
    depth_index = lax.axis_index("depth")
    depth_count = lax.axis_size("depth")
    wave = lax.axis_index("wave")
    slices = phase_shift.shape[0]
    rows, cols = incident.shape[2], incident.shape[3]
    reach = HALF * slices
    assert reach <= rows and reach <= cols

    trans_own = transmission(phase_shift, absorption)
    illum = incident.shape[0]
    width = cols + reach
    tall = rows + 2 * reach
    band = toeplitz(kernel, max(tall, width), HALF)
    (field_grown, trans_grown), band = grow(
        jnp.concatenate([incident.reshape(2 * illum, rows, cols), trans_own.reshape(2 * slices, rows, cols)]),
        reach,
        (2 * illum, 2 * slices),
        band,
    )
    first_field = field_grown.reshape(illum, 2, rows + 2 * reach, cols + reach)
    trans_reg = trans_grown.reshape(slices, 2, rows + 2 * reach, cols + reach)
    natural = band[:, :, :width, :width]
    turned = jnp.concatenate([natural[:, :, reach:], jnp.flip(natural[:, :, :reach], axis=2)], axis=2)
    turned = jnp.concatenate([turned[..., reach:], jnp.flip(turned[..., :reach], axis=3)], axis=3)
    col_band = jnp.where(wave == 0, natural, turned)
    row_bands = [
        band[:, :, HALF * (s + 1): tall - HALF * (s + 1), HALF * s: tall - HALF * s]
        for s in range(slices)
    ]

    def depth_section(field):
        current = field
        for s in range(slices):
            keep = width - HALF * s
            moved = modulate(current, trans_reg[s, :, HALF * s: tall - HALF * s, :keep])
            rows_done = jnp.einsum(
                "dcab,icbj->idaj", row_bands[s], moved, precision=lax.Precision.HIGH
            )
            current = jnp.einsum(
                "dcyj,icxj->idxy",
                col_band[:, :, : keep - HALF, :keep],
                rows_done,
                precision=lax.Precision.HIGH,
            )
        return current

    exits = jnp.zeros(incident.shape, jnp.float32)
    tiles = lax.axis_size("tile")
    spot = lambda t, d: t * depth_count + d
    ahead = range(depth_count - 1)
    own_pairs = [(spot(t, d), spot(t, d + 1)) for t in range(tiles) for d in ahead]
    prev_pairs = [(spot(t - 1, d), spot(t, d + 1)) for t in range(1, tiles) for d in ahead]
    next_pairs = [(spot(t + 1, d), spot(t, d + 1)) for t in range(tiles - 1) for d in ahead]
    field = first_field
    for step in range(depth_count):
        result = depth_section(field)
        exits = jnp.where(depth_index == step, result, exits)
        if step + 1 < depth_count:
            flat = result.reshape(2 * illum, rows, cols)
            grid = ("tile", "depth")
            from_prev = lax.ppermute(flat[:, rows - reach:], grid, prev_pairs)
            mine = lax.ppermute(flat, grid, own_pairs)
            from_next = lax.ppermute(flat[:, :reach], grid, next_pairs)
            field = widen(jnp.concatenate([from_prev, mine, from_next], axis=1), reach, (2 * illum,))[0].reshape(
                illum, 2, tall, width
            )
    return exits[None]


def solution(mesh):
    return jax.shard_map(
        per_device,
        mesh=mesh,
        in_specs=(
            P(None, None, ("groups", "tile"), "wave"),
            P("depth", ("groups", "tile"), "wave"),
            P("depth", ("groups", "tile"), "wave"),
            P(),
        ),
        out_specs=P("depth", None, None, ("groups", "tile"), "wave"),
        check_vma=False,
    )
```

```python
import jax
import jax.numpy as jnp
from jax import lax
from jax.sharding import PartitionSpec as P

TAPS = 33
HALF = 16


def toeplitz(kernel, size, shift):
    period = 2 * size
    gap = jnp.zeros((2, period - TAPS), jnp.float32)
    base = jnp.concatenate([kernel[:, shift:], gap, kernel[:, :shift]], axis=1)
    rolled = jnp.tile(base, (1, size))[:, : size * (period - 1)]
    bands = rolled.reshape(2, size, period - 1)[:, :, :size]
    band_real, band_imag = bands[0], bands[1]
    top = jnp.stack([band_real, -band_imag], axis=0)
    bottom = jnp.stack([band_imag, band_real], axis=0)
    return jnp.stack([top, bottom], axis=0)


def transmission(phase_part, absorb_part):
    amplitude = jnp.exp(-absorb_part.astype(jnp.float32))
    angle_part = phase_part.astype(jnp.float32)
    return jnp.stack([amplitude * jnp.cos(angle_part), amplitude * jnp.sin(angle_part)], axis=-3)


def modulate(field, trans):
    field_real = field[:, 0]
    field_imag = field[:, 1]
    return jnp.stack(
        [
            field_real * trans[0] - field_imag * trans[1],
            field_real * trans[1] + field_imag * trans[0],
        ],
        axis=1,
    )


def grow(stack, halo, splits, rider, needs=None):
    tiles = lax.axis_size("tile")
    rows, cols = stack.shape[-2], stack.shape[-1]
    needs = [halo] * stack.shape[0] if needs is None else needs
    slabs, places = [], []
    for c in sorted(range(len(needs)), key=lambda c: -needs[c]):
        for n, used in enumerate(slabs):
            if used + needs[c] <= halo:
                places.append((c, n, used))
                slabs[n] += needs[c]
                break
        else:
            places.append((c, len(slabs), 0))
            slabs.append(needs[c])

    def pack(take):
        bins = [[] for _ in slabs]
        for c, n, _ in places:
            bins[n].append(take(c))
        return jnp.stack([
            jnp.concatenate(b + [jnp.zeros((halo - used, cols), stack.dtype)] * (used < halo), axis=0)
            for b, used in zip(bins, slabs)
        ])

    sent_prev = pack(lambda c: stack[c, rows - needs[c]:])
    sent_next = pack(lambda c: stack[c, :needs[c]])
    from_prev = lax.ppermute(sent_prev, "tile", [(i, i + 1) for i in range(tiles - 1)])
    from_next = lax.ppermute(sent_next, "tile", [(i + 1, i) for i in range(tiles - 1)])
    columns = [None] * len(needs)
    for c, n, at in places:
        gap = [jnp.zeros((halo - needs[c], cols), stack.dtype)] * (needs[c] < halo)
        columns[c] = jnp.concatenate(
            gap + [from_prev[n, at:at + needs[c]], stack[c], from_next[n, at:at + needs[c]]] + gap,
            axis=0,
        )
    tall = jnp.stack(columns)
    rider, tall = lax.optimization_barrier((rider, tall))
    return widen(tall, halo, splits), rider


def widen(tall, halo, splits):
    wave = lax.axis_index("wave")
    cols = tall.shape[-1]
    got = lax.ppermute(tall, "wave", [(0, 1), (1, 0)])
    out, start = [], 0
    for size in splits:
        own, other = tall[start:start + size], got[start:start + size]
        start += size
        left = jnp.concatenate([own, other[..., :halo]], axis=-1)
        right = jnp.concatenate([other[..., cols - halo:], own], axis=-1)
        out.append(jnp.where(wave == 0, left, right))
    return out


def per_device(incident, phase_shift, absorption, fir_taps):
    kernel = fir_taps / jnp.sqrt(jnp.sum(fir_taps * fir_taps) + 1e-06)
    depth_index = lax.axis_index("depth")
    depth_count = lax.axis_size("depth")
    wave = lax.axis_index("wave")
    slices = phase_shift.shape[0]
    rows, cols = incident.shape[2], incident.shape[3]
    reach = HALF * slices
    assert reach <= rows and reach <= cols

    trans_own = transmission(phase_shift, absorption)
    illum = incident.shape[0]
    width = cols + reach
    tall = rows + 2 * reach
    band = toeplitz(kernel, max(tall, width), HALF)
    (field_grown, trans_grown), band = grow(
        jnp.concatenate([incident.reshape(2 * illum, rows, cols), trans_own.reshape(2 * slices, rows, cols)]),
        reach,
        (2 * illum, 2 * slices),
        band,
        [reach] * (2 * illum) + [reach - HALF * s for s in range(slices) for _ in range(2)],
    )
    first_field = field_grown.reshape(illum, 2, rows + 2 * reach, cols + reach)
    trans_reg = trans_grown.reshape(slices, 2, rows + 2 * reach, cols + reach)
    col_band = band[:, :, :width, :width]
    row_bands = [
        band[:, :, HALF * (s + 1): tall - HALF * (s + 1), HALF * s: tall - HALF * s]
        for s in range(slices)
    ]

    last_band = jnp.where(wave == 0, col_band[:, :, :cols], col_band[:, :, reach:reach + cols])

    def depth_section(field):
        current = field
        for s in range(slices):
            moved = modulate(current, trans_reg[s, :, HALF * s: tall - HALF * s])
            rows_done = jnp.einsum(
                "dcab,icbj->idaj", row_bands[s], moved, precision=lax.Precision.HIGH
            )
            current = jnp.einsum(
                "dcyj,icxj->idxy",
                last_band if s == slices - 1 else col_band,
                rows_done,
                precision=lax.Precision.HIGH,
            )
        return current

    exits = jnp.zeros(incident.shape, jnp.float32)
    tiles = lax.axis_size("tile")
    spot = lambda t, d: t * depth_count + d
    ahead = range(depth_count - 1)
    own_pairs = [(spot(t, d), spot(t, d + 1)) for t in range(tiles) for d in ahead]
    prev_pairs = [(spot(t - 1, d), spot(t, d + 1)) for t in range(1, tiles) for d in ahead]
    next_pairs = [(spot(t + 1, d), spot(t, d + 1)) for t in range(tiles - 1) for d in ahead]
    field = first_field
    for step in range(depth_count):
        result = depth_section(field)
        exits = jnp.where(depth_index == step, result, exits)
        if step + 1 < depth_count:
            flat = result.reshape(2 * illum, rows, cols)
            grid = ("tile", "depth")
            from_prev = lax.ppermute(flat[:, rows - reach:], grid, prev_pairs)
            mine = lax.ppermute(flat, grid, own_pairs)
            from_next = lax.ppermute(flat[:, :reach], grid, next_pairs)
            field = widen(jnp.concatenate([from_prev, mine, from_next], axis=1), reach, (2 * illum,))[0].reshape(
                illum, 2, tall, width
            )
    return exits[None]


def solution(mesh):
    return jax.shard_map(
        per_device,
        mesh=mesh,
        in_specs=(
            P(None, None, ("groups", "tile"), "wave"),
            P("depth", ("groups", "tile"), "wave"),
            P("depth", ("groups", "tile"), "wave"),
            P(),
        ),
        out_specs=P("depth", None, None, ("groups", "tile"), "wave"),
        check_vma=False,
    )
```

```python
import jax
import jax.numpy as jnp
from jax import lax
from jax.sharding import PartitionSpec as P

TAPS = 33
HALF = 16


def toeplitz(kernel, size, shift):
    period = 2 * size
    gap = jnp.zeros((2, period - TAPS), jnp.float32)
    base = jnp.concatenate([kernel[:, shift:], gap, kernel[:, :shift]], axis=1)
    rolled = jnp.tile(base, (1, size))[:, : size * (period - 1)]
    bands = rolled.reshape(2, size, period - 1)[:, :, :size]
    band_real, band_imag = bands[0], bands[1]
    top = jnp.stack([band_real, -band_imag], axis=0)
    bottom = jnp.stack([band_imag, band_real], axis=0)
    return jnp.stack([top, bottom], axis=0)


def transmission(phase_part, absorb_part):
    amplitude = jnp.exp(-absorb_part.astype(jnp.float32))
    angle_part = phase_part.astype(jnp.float32)
    return jnp.stack([amplitude * jnp.cos(angle_part), amplitude * jnp.sin(angle_part)], axis=-3)


def modulate(field, trans):
    field_real = field[:, 0]
    field_imag = field[:, 1]
    return jnp.stack(
        [
            field_real * trans[0] - field_imag * trans[1],
            field_real * trans[1] + field_imag * trans[0],
        ],
        axis=1,
    )


def grow(stack, halo, splits, rider, needs=None):
    tiles = lax.axis_size("tile")
    rows, cols = stack.shape[-2], stack.shape[-1]
    needs = [halo] * stack.shape[0] if needs is None else needs
    slabs, places = [], []
    for c in sorted(range(len(needs)), key=lambda c: -needs[c]):
        for n, used in enumerate(slabs):
            if used + needs[c] <= halo:
                places.append((c, n, used))
                slabs[n] += needs[c]
                break
        else:
            places.append((c, len(slabs), 0))
            slabs.append(needs[c])

    def pack(take):
        bins = [[] for _ in slabs]
        for c, n, _ in places:
            bins[n].append(take(c))
        return jnp.stack([
            jnp.concatenate(b + [jnp.zeros((halo - used, cols), stack.dtype)] * (used < halo), axis=0)
            for b, used in zip(bins, slabs)
        ])

    sent_prev = pack(lambda c: stack[c, rows - needs[c]:])
    sent_next = pack(lambda c: stack[c, :needs[c]])
    from_prev = lax.ppermute(sent_prev, "tile", [(i, i + 1) for i in range(tiles - 1)])
    from_next = lax.ppermute(sent_next, "tile", [(i + 1, i) for i in range(tiles - 1)])
    columns = [None] * len(needs)
    for c, n, at in places:
        gap = [jnp.zeros((halo - needs[c], cols), stack.dtype)] * (needs[c] < halo)
        columns[c] = jnp.concatenate(
            gap + [from_prev[n, at:at + needs[c]], stack[c], from_next[n, at:at + needs[c]]] + gap,
            axis=0,
        )
    tall = jnp.stack(columns)
    rider, tall = lax.optimization_barrier((rider, tall))
    return widen(tall, halo, splits), rider


def widen(tall, halo, splits):
    wave = lax.axis_index("wave")
    count, cols = tall.shape[0], tall.shape[-1]
    if 2 * halo == cols:
        if count % 2:
            tall = jnp.concatenate([tall, jnp.zeros_like(tall[:1])])
        half = tall.shape[0] // 2
        slabs = jnp.where(
            wave == 0,
            jnp.concatenate([tall[:half, :, halo:], tall[half:, :, halo:]], axis=-1),
            jnp.concatenate([tall[:half, :, :halo], tall[half:, :, :halo]], axis=-1),
        )
        got = lax.ppermute(slabs, "wave", [(0, 1), (1, 0)])
        parts = jnp.concatenate([got[..., :halo], got[..., halo:]], axis=0)
    else:
        got = lax.ppermute(tall, "wave", [(0, 1), (1, 0)])
        parts = jnp.where(wave == 0, got[..., :halo], got[..., cols - halo:])
    out, start = [], 0
    for size in splits:
        own, part = tall[start:start + size], parts[start:start + size]
        start += size
        left = jnp.concatenate([own, part], axis=-1)
        right = jnp.concatenate([part, own], axis=-1)
        out.append(jnp.where(wave == 0, left, right))
    return out


def per_device(incident, phase_shift, absorption, fir_taps):
    kernel = fir_taps / jnp.sqrt(jnp.sum(fir_taps * fir_taps) + 1e-06)
    depth_index = lax.axis_index("depth")
    depth_count = lax.axis_size("depth")
    wave = lax.axis_index("wave")
    slices = phase_shift.shape[0]
    rows, cols = incident.shape[2], incident.shape[3]
    reach = HALF * slices
    assert reach <= rows and reach <= cols

    trans_own = transmission(phase_shift, absorption)
    illum = incident.shape[0]
    width = cols + reach
    tall = rows + 2 * reach
    band = toeplitz(kernel, max(tall, width), HALF)
    (field_grown, trans_grown), band = grow(
        jnp.concatenate([incident.reshape(2 * illum, rows, cols), trans_own.reshape(2 * slices, rows, cols)]),
        reach,
        (2 * illum, 2 * slices),
        band,
        [reach] * (2 * illum) + [reach - HALF * s for s in range(slices) for _ in range(2)],
    )
    first_field = field_grown.reshape(illum, 2, rows + 2 * reach, cols + reach)
    trans_reg = trans_grown.reshape(slices, 2, rows + 2 * reach, cols + reach)
    col_band = band[:, :, :width, :width]
    row_bands = [
        band[:, :, HALF * (s + 1): tall - HALF * (s + 1), HALF * s: tall - HALF * s]
        for s in range(slices)
    ]

    last_band = jnp.where(wave == 0, col_band[:, :, :cols], col_band[:, :, reach:reach + cols])

    def depth_section(field):
        current = field
        for s in range(slices):
            moved = modulate(current, trans_reg[s, :, HALF * s: tall - HALF * s])
            rows_done = jnp.einsum(
                "dcab,icbj->idaj", row_bands[s], moved, precision=lax.Precision.HIGH
            )
            current = jnp.einsum(
                "dcyj,icxj->idxy",
                last_band if s == slices - 1 else col_band,
                rows_done,
                precision=lax.Precision.HIGH,
            )
        return current

    exits = jnp.zeros(incident.shape, jnp.float32)
    tiles = lax.axis_size("tile")
    spot = lambda t, d: t * depth_count + d
    ahead = range(depth_count - 1)
    own_pairs = [(spot(t, d), spot(t, d + 1)) for t in range(tiles) for d in ahead]
    prev_pairs = [(spot(t - 1, d), spot(t, d + 1)) for t in range(1, tiles) for d in ahead]
    next_pairs = [(spot(t + 1, d), spot(t, d + 1)) for t in range(tiles - 1) for d in ahead]
    field = first_field
    for step in range(depth_count):
        result = depth_section(field)
        exits = jnp.where(depth_index == step, result, exits)
        if step + 1 < depth_count:
            flat = result.reshape(2 * illum, rows, cols)
            grid = ("tile", "depth")
            from_prev = lax.ppermute(flat[:, rows - reach:], grid, prev_pairs)
            mine = lax.ppermute(flat, grid, own_pairs)
            from_next = lax.ppermute(flat[:, :reach], grid, next_pairs)
            field = widen(jnp.concatenate([from_prev, mine, from_next], axis=1), reach, (2 * illum,))[0].reshape(
                illum, 2, tall, width
            )
    return exits[None]


def solution(mesh):
    return jax.shard_map(
        per_device,
        mesh=mesh,
        in_specs=(
            P(None, None, ("groups", "tile"), "wave"),
            P("depth", ("groups", "tile"), "wave"),
            P("depth", ("groups", "tile"), "wave"),
            P(),
        ),
        out_specs=P("depth", None, None, ("groups", "tile"), "wave"),
        check_vma=False,
    )
```

```python
import jax
import jax.numpy as jnp
from jax import lax
from jax.sharding import PartitionSpec as P

TAPS = 33
HALF = 16


def toeplitz(kernel, size, shift):
    period = 2 * size
    gap = jnp.zeros((2, period - TAPS), jnp.float32)
    base = jnp.concatenate([kernel[:, shift:], gap, kernel[:, :shift]], axis=1)
    rolled = jnp.tile(base, (1, size))[:, : size * (period - 1)]
    bands = rolled.reshape(2, size, period - 1)[:, :, :size]
    band_real, band_imag = bands[0], bands[1]
    top = jnp.stack([band_real, -band_imag], axis=0)
    bottom = jnp.stack([band_imag, band_real], axis=0)
    return jnp.stack([top, bottom], axis=0)


def transmission(phase_part, absorb_part):
    amplitude = jnp.exp(-absorb_part.astype(jnp.float32))
    angle_part = phase_part.astype(jnp.float32)
    return jnp.stack([amplitude * jnp.cos(angle_part), amplitude * jnp.sin(angle_part)], axis=-3)


def modulate(field, trans):
    field_real = field[:, 0]
    field_imag = field[:, 1]
    return jnp.stack(
        [
            field_real * trans[0] - field_imag * trans[1],
            field_real * trans[1] + field_imag * trans[0],
        ],
        axis=1,
    )


def grow(stack, halo, splits, rider, needs=None):
    tiles = lax.axis_size("tile")
    rows, cols = stack.shape[-2], stack.shape[-1]
    needs = [halo] * stack.shape[0] if needs is None else needs
    slabs, places = [], []
    for c in sorted(range(len(needs)), key=lambda c: -needs[c]):
        for n, used in enumerate(slabs):
            if used + needs[c] <= halo:
                places.append((c, n, used))
                slabs[n] += needs[c]
                break
        else:
            places.append((c, len(slabs), 0))
            slabs.append(needs[c])

    def pack(take):
        bins = [[] for _ in slabs]
        for c, n, _ in places:
            bins[n].append(take(c))
        return jnp.stack([
            jnp.concatenate(b + [jnp.zeros((halo - used, cols), stack.dtype)] * (used < halo), axis=0)
            for b, used in zip(bins, slabs)
        ])

    sent_prev = pack(lambda c: stack[c, rows - needs[c]:])
    sent_next = pack(lambda c: stack[c, :needs[c]])
    from_prev = lax.ppermute(sent_prev, "tile", [(i, i + 1) for i in range(tiles - 1)])
    from_next = lax.ppermute(sent_next, "tile", [(i + 1, i) for i in range(tiles - 1)])
    columns = [None] * len(needs)
    for c, n, at in places:
        gap = [jnp.zeros((halo - needs[c], cols), stack.dtype)] * (needs[c] < halo)
        columns[c] = jnp.concatenate(
            gap + [from_prev[n, at:at + needs[c]], stack[c], from_next[n, at:at + needs[c]]] + gap,
            axis=0,
        )
    tall = jnp.stack(columns)
    rider, tall = lax.optimization_barrier((rider, tall))
    return widen(tall, halo, splits), rider


def widen(tall, halo, splits):
    wave = lax.axis_index("wave")
    count, cols = tall.shape[0], tall.shape[-1]
    if 2 * halo == cols:
        if count % 2:
            tall = jnp.concatenate([tall, jnp.zeros_like(tall[:1])])
        half = tall.shape[0] // 2
        slabs = jnp.where(
            wave == 0,
            jnp.concatenate([tall[:half, :, halo:], tall[half:, :, halo:]], axis=-1),
            jnp.concatenate([tall[:half, :, :halo], tall[half:, :, :halo]], axis=-1),
        )
        got = lax.ppermute(slabs, "wave", [(0, 1), (1, 0)])
        parts = jnp.concatenate([got[..., :halo], got[..., halo:]], axis=0)
    else:
        got = lax.ppermute(tall, "wave", [(0, 1), (1, 0)])
        parts = jnp.where(wave == 0, got[..., :halo], got[..., cols - halo:])
    out, start = [], 0
    for size in splits:
        own, part = tall[start:start + size], parts[start:start + size]
        start += size
        left = jnp.concatenate([own, part], axis=-1)
        right = jnp.concatenate([part, own], axis=-1)
        out.append(jnp.where(wave == 0, left, right))
    return out


def per_device(incident, phase_shift, absorption, fir_taps):
    kernel = fir_taps / jnp.sqrt(jnp.sum(fir_taps * fir_taps) + 1e-06)
    depth_index = lax.axis_index("depth")
    depth_count = lax.axis_size("depth")
    wave = lax.axis_index("wave")
    slices = phase_shift.shape[0]
    rows, cols = incident.shape[2], incident.shape[3]
    reach = HALF * slices
    assert reach <= rows and reach <= cols

    trans_own = transmission(phase_shift, absorption)
    illum = incident.shape[0]
    width = cols + reach
    tall = rows + 2 * reach
    band = toeplitz(kernel, max(tall, width), HALF)
    (field_grown, trans_grown), band = grow(
        jnp.concatenate([incident.reshape(2 * illum, rows, cols), trans_own.reshape(2 * slices, rows, cols)]),
        reach,
        (2 * illum, 2 * slices),
        band,
        [reach] * (2 * illum) + [reach - HALF * s for s in range(slices) for _ in range(2)],
    )
    first_field = field_grown.reshape(illum, 2, rows + 2 * reach, cols + reach)
    trans_reg = trans_grown.reshape(slices, 2, rows + 2 * reach, cols + reach)
    col_band = band[:, :, :width, :width]
    spans, start, length = [], 0, tall
    for s in range(slices):
        exact = tall - 2 * HALF * (s + 1)
        margin = 8 if exact % 128 == 0 and s + 1 < slices else 0
        spans.append((start, length, HALF * (s + 1) - margin, exact + 2 * margin))
        start, length = spans[-1][2], spans[-1][3]
    row_bands = [band[:, :, o: o + n, i: i + m] for i, m, o, n in spans]

    last_band = jnp.where(wave == 0, col_band[:, :, :cols], col_band[:, :, reach:reach + cols])

    def depth_section(field):
        current = field
        for s in range(slices):
            moved = modulate(current, trans_reg[s, :, spans[s][0]: spans[s][0] + spans[s][1]])
            rows_done = jnp.einsum(
                "dcab,icbj->idaj", row_bands[s], moved, precision=lax.Precision.HIGH
            )
            current = jnp.einsum(
                "dcyj,icxj->idxy",
                last_band if s == slices - 1 else col_band,
                rows_done,
                precision=lax.Precision.HIGH,
            )
        return current

    exits = jnp.zeros(incident.shape, jnp.float32)
    tiles = lax.axis_size("tile")
    spot = lambda t, d: t * depth_count + d
    ahead = range(depth_count - 1)
    own_pairs = [(spot(t, d), spot(t, d + 1)) for t in range(tiles) for d in ahead]
    prev_pairs = [(spot(t - 1, d), spot(t, d + 1)) for t in range(1, tiles) for d in ahead]
    next_pairs = [(spot(t + 1, d), spot(t, d + 1)) for t in range(tiles - 1) for d in ahead]
    field = first_field
    for step in range(depth_count):
        result = depth_section(field)
        exits = jnp.where(depth_index == step, result, exits)
        if step + 1 < depth_count:
            flat = result.reshape(2 * illum, rows, cols)
            grid = ("tile", "depth")
            from_prev = lax.ppermute(flat[:, rows - reach:], grid, prev_pairs)
            mine = lax.ppermute(flat, grid, own_pairs)
            from_next = lax.ppermute(flat[:, :reach], grid, next_pairs)
            field = widen(jnp.concatenate([from_prev, mine, from_next], axis=1), reach, (2 * illum,))[0].reshape(
                illum, 2, tall, width
            )
    return exits[None]


def solution(mesh):
    return jax.shard_map(
        per_device,
        mesh=mesh,
        in_specs=(
            P(None, None, ("groups", "tile"), "wave"),
            P("depth", ("groups", "tile"), "wave"),
            P("depth", ("groups", "tile"), "wave"),
            P(),
        ),
        out_specs=P("depth", None, None, ("groups", "tile"), "wave"),
        check_vma=False,
    )
```

```python
import jax
import jax.numpy as jnp
from jax import lax
from jax.sharding import PartitionSpec as P

TAPS = 33
HALF = 16


def toeplitz(kernel, size, shift):
    period = 2 * size
    gap = jnp.zeros((2, period - TAPS), jnp.float32)
    base = jnp.concatenate([kernel[:, shift:], gap, kernel[:, :shift]], axis=1)
    rolled = jnp.tile(base, (1, size))[:, : size * (period - 1)]
    bands = rolled.reshape(2, size, period - 1)[:, :, :size]
    band_real, band_imag = bands[0], bands[1]
    top = jnp.stack([band_real, -band_imag], axis=0)
    bottom = jnp.stack([band_imag, band_real], axis=0)
    return jnp.stack([top, bottom], axis=0)


def transmission(phase_part, absorb_part):
    amplitude = jnp.exp(-absorb_part.astype(jnp.float32))
    angle_part = phase_part.astype(jnp.float32)
    return jnp.stack([amplitude * jnp.cos(angle_part), amplitude * jnp.sin(angle_part)], axis=-3)


def modulate(field, trans):
    field_real = field[:, 0]
    field_imag = field[:, 1]
    return jnp.stack(
        [
            field_real * trans[0] - field_imag * trans[1],
            field_real * trans[1] + field_imag * trans[0],
        ],
        axis=1,
    )


def grow(stack, halo, splits, rider, needs=None):
    tiles = lax.axis_size("tile")
    rows, cols = stack.shape[-2], stack.shape[-1]
    needs = [halo] * stack.shape[0] if needs is None else needs
    slabs, places = [], []
    for c in sorted(range(len(needs)), key=lambda c: -needs[c]):
        for n, used in enumerate(slabs):
            if used + needs[c] <= halo:
                places.append((c, n, used))
                slabs[n] += needs[c]
                break
        else:
            places.append((c, len(slabs), 0))
            slabs.append(needs[c])

    def pack(take):
        bins = [[] for _ in slabs]
        for c, n, _ in places:
            bins[n].append(take(c))
        return jnp.stack([
            jnp.concatenate(b + [jnp.zeros((halo - used, cols), stack.dtype)] * (used < halo), axis=0)
            for b, used in zip(bins, slabs)
        ])

    sent_prev = pack(lambda c: stack[c, rows - needs[c]:])
    sent_next = pack(lambda c: stack[c, :needs[c]])
    from_prev = lax.ppermute(sent_prev, "tile", [(i, i + 1) for i in range(tiles - 1)])
    from_next = lax.ppermute(sent_next, "tile", [(i + 1, i) for i in range(tiles - 1)])
    columns = [None] * len(needs)
    for c, n, at in places:
        gap = [jnp.zeros((halo - needs[c], cols), stack.dtype)] * (needs[c] < halo)
        columns[c] = jnp.concatenate(
            gap + [from_prev[n, at:at + needs[c]], stack[c], from_next[n, at:at + needs[c]]] + gap,
            axis=0,
        )
    tall = jnp.stack(columns)
    rider, tall = lax.optimization_barrier((rider, tall))
    return widen(tall, halo, splits), rider


def widen(tall, halo, splits):
    wave = lax.axis_index("wave")
    count, cols = tall.shape[0], tall.shape[-1]
    if 2 * halo == cols:
        if count % 2:
            tall = jnp.concatenate([tall, jnp.zeros_like(tall[:1])])
        half = tall.shape[0] // 2
        slabs = jnp.where(
            wave == 0,
            jnp.concatenate([tall[:half, :, halo:], tall[half:, :, halo:]], axis=-1),
            jnp.concatenate([tall[:half, :, :halo], tall[half:, :, :halo]], axis=-1),
        )
        got = lax.ppermute(slabs, "wave", [(0, 1), (1, 0)])
        parts = jnp.concatenate([got[..., :halo], got[..., halo:]], axis=0)
    else:
        got = lax.ppermute(tall, "wave", [(0, 1), (1, 0)])
        parts = jnp.where(wave == 0, got[..., :halo], got[..., cols - halo:])
    out, start = [], 0
    for size in splits:
        own, part = tall[start:start + size], parts[start:start + size]
        start += size
        left = jnp.concatenate([own, part], axis=-1)
        right = jnp.concatenate([part, own], axis=-1)
        out.append(jnp.where(wave == 0, left, right))
    return out


def per_device(incident, phase_shift, absorption, fir_taps):
    kernel = fir_taps / jnp.sqrt(jnp.sum(fir_taps * fir_taps) + 1e-06)
    depth_index = lax.axis_index("depth")
    depth_count = lax.axis_size("depth")
    wave = lax.axis_index("wave")
    slices = phase_shift.shape[0]
    rows, cols = incident.shape[2], incident.shape[3]
    reach = HALF * slices
    assert reach <= rows and reach <= cols

    trans_own = transmission(phase_shift, absorption)
    illum = incident.shape[0]
    width = cols + reach
    tall = rows + 2 * reach
    band = toeplitz(kernel, max(tall, width), HALF)
    (field_grown, trans_grown), band = grow(
        jnp.concatenate([incident.reshape(2 * illum, rows, cols), trans_own.reshape(2 * slices, rows, cols)]),
        reach,
        (2 * illum, 2 * slices),
        band,
        [reach] * (2 * illum) + [reach - HALF * s for s in range(slices) for _ in range(2)],
    )
    first_field = field_grown.reshape(illum, 2, rows + 2 * reach, cols + reach)
    trans_reg = trans_grown.reshape(slices, 2, rows + 2 * reach, cols + reach)
    col_band = band[:, :, :width, :width]
    row_bands = [
        band[:, :, HALF * (s + 1): tall - HALF * (s + 1), HALF * s: tall - HALF * s]
        for s in range(slices)
    ]

    last_band = jnp.where(wave == 0, col_band[:, :, :cols], col_band[:, :, reach:reach + cols])

    def depth_section(field):
        current = field
        for s in range(slices):
            moved = modulate(current, trans_reg[s, :, HALF * s: tall - HALF * s])
            rows_done = jnp.einsum(
                "dcab,icbj->idaj", row_bands[s], moved, precision=lax.Precision.HIGH
            )
            current = jnp.einsum(
                "dcyj,icxj->idxy",
                last_band if s == slices - 1 else col_band,
                rows_done,
                precision=lax.Precision.HIGH,
            )
        return current

    exits = jnp.zeros(incident.shape, jnp.float32)
    tiles = lax.axis_size("tile")
    spot = lambda t, d: t * depth_count + d
    ahead = range(depth_count - 1)
    own_pairs = [(spot(t, d), spot(t, d + 1)) for t in range(tiles) for d in ahead]
    prev_pairs = [(spot(t - 1, d), spot(t, d + 1)) for t in range(1, tiles) for d in ahead]
    next_pairs = [(spot(t + 1, d), spot(t, d + 1)) for t in range(tiles - 1) for d in ahead]
    field = first_field
    for step in range(depth_count):
        result = lax.optimization_barrier(depth_section(field))
        exits = jnp.where(depth_index == step, result, exits)
        if step + 1 < depth_count:
            flat = result.reshape(2 * illum, rows, cols)
            grid = ("tile", "depth")
            from_prev = lax.ppermute(flat[:, rows - reach:], grid, prev_pairs)
            mine = lax.ppermute(flat, grid, own_pairs)
            from_next = lax.ppermute(flat[:, :reach], grid, next_pairs)
            field = widen(jnp.concatenate([from_prev, mine, from_next], axis=1), reach, (2 * illum,))[0].reshape(
                illum, 2, tall, width
            )
    return exits[None]


def solution(mesh):
    return jax.shard_map(
        per_device,
        mesh=mesh,
        in_specs=(
            P(None, None, ("groups", "tile"), "wave"),
            P("depth", ("groups", "tile"), "wave"),
            P("depth", ("groups", "tile"), "wave"),
            P(),
        ),
        out_specs=P("depth", None, None, ("groups", "tile"), "wave"),
        check_vma=False,
    )
```

```python
import jax
import jax.numpy as jnp
from jax import lax
from jax.sharding import PartitionSpec as P

TAPS = 33
HALF = 16


def toeplitz(kernel, size, shift):
    period = 2 * size
    gap = jnp.zeros((2, period - TAPS), jnp.float32)
    base = jnp.concatenate([kernel[:, shift:], gap, kernel[:, :shift]], axis=1)
    rolled = jnp.tile(base, (1, size))[:, : size * (period - 1)]
    bands = rolled.reshape(2, size, period - 1)[:, :, :size]
    band_real, band_imag = bands[0], bands[1]
    top = jnp.stack([band_real, -band_imag], axis=0)
    bottom = jnp.stack([band_imag, band_real], axis=0)
    return jnp.stack([top, bottom], axis=0)


def transmission(phase_part, absorb_part):
    amplitude = jnp.exp(-absorb_part.astype(jnp.float32))
    angle_part = phase_part.astype(jnp.float32)
    return jnp.stack([amplitude * jnp.cos(angle_part), amplitude * jnp.sin(angle_part)], axis=-3)


def modulate(field, trans):
    field_real = field[:, 0]
    field_imag = field[:, 1]
    return jnp.stack(
        [
            field_real * trans[0] - field_imag * trans[1],
            field_real * trans[1] + field_imag * trans[0],
        ],
        axis=1,
    )


def grow(stack, halo, splits, rider, needs=None):
    tiles = lax.axis_size("tile")
    rows, cols = stack.shape[-2], stack.shape[-1]
    needs = [halo] * stack.shape[0] if needs is None else needs
    slabs, places = [], []
    for c in sorted(range(len(needs)), key=lambda c: -needs[c]):
        for n, used in enumerate(slabs):
            if used + needs[c] <= halo:
                places.append((c, n, used))
                slabs[n] += needs[c]
                break
        else:
            places.append((c, len(slabs), 0))
            slabs.append(needs[c])

    def pack(take):
        bins = [[] for _ in slabs]
        for c, n, _ in places:
            bins[n].append(take(c))
        return jnp.stack([
            jnp.concatenate(b + [jnp.zeros((halo - used, cols), stack.dtype)] * (used < halo), axis=0)
            for b, used in zip(bins, slabs)
        ])

    sent_prev = pack(lambda c: stack[c, rows - needs[c]:])
    sent_next = pack(lambda c: stack[c, :needs[c]])
    from_prev = lax.ppermute(sent_prev, "tile", [(i, i + 1) for i in range(tiles - 1)])
    from_next = lax.ppermute(sent_next, "tile", [(i + 1, i) for i in range(tiles - 1)])
    columns = [None] * len(needs)
    for c, n, at in places:
        gap = [jnp.zeros((halo - needs[c], cols), stack.dtype)] * (needs[c] < halo)
        columns[c] = jnp.concatenate(
            gap + [from_prev[n, at:at + needs[c]], stack[c], from_next[n, at:at + needs[c]]] + gap,
            axis=0,
        )
    tall = jnp.stack(columns)
    rider, tall = lax.optimization_barrier((rider, tall))
    return widen(tall, halo, splits), rider


def widen(tall, halo, splits):
    wave = lax.axis_index("wave")
    count, cols = tall.shape[0], tall.shape[-1]
    if 2 * halo == cols:
        if count % 2:
            tall = jnp.concatenate([tall, jnp.zeros_like(tall[:1])])
        half = tall.shape[0] // 2
        slabs = jnp.where(
            wave == 0,
            jnp.concatenate([tall[:half, :, halo:], tall[half:, :, halo:]], axis=-1),
            jnp.concatenate([tall[:half, :, :halo], tall[half:, :, :halo]], axis=-1),
        )
        got = lax.ppermute(slabs, "wave", [(0, 1), (1, 0)])
        parts = jnp.concatenate([got[..., :halo], got[..., halo:]], axis=0)
    else:
        got = lax.ppermute(tall, "wave", [(0, 1), (1, 0)])
        parts = jnp.where(wave == 0, got[..., :halo], got[..., cols - halo:])
    out, start = [], 0
    for size in splits:
        own, part = tall[start:start + size], parts[start:start + size]
        start += size
        left = jnp.concatenate([own, part], axis=-1)
        right = jnp.concatenate([part, own], axis=-1)
        out.append(jnp.where(wave == 0, left, right))
    return out


def per_device(incident, phase_shift, absorption, fir_taps):
    kernel = fir_taps / jnp.sqrt(jnp.sum(fir_taps * fir_taps) + 1e-06)
    depth_index = lax.axis_index("depth")
    depth_count = lax.axis_size("depth")
    wave = lax.axis_index("wave")
    slices = phase_shift.shape[0]
    rows, cols = incident.shape[2], incident.shape[3]
    reach = HALF * slices
    assert reach <= rows and reach <= cols

    trans_own = transmission(phase_shift, absorption)
    illum = incident.shape[0]
    width = cols + reach
    tall = rows + 2 * reach
    band = toeplitz(kernel, max(tall, width), HALF)
    (field_grown, trans_grown), band = grow(
        jnp.concatenate([incident.reshape(2 * illum, rows, cols), trans_own.reshape(2 * slices, rows, cols)]),
        reach,
        (2 * illum, 2 * slices),
        band,
        [reach] * (2 * illum) + [reach - HALF * s for s in range(slices) for _ in range(2)],
    )
    first_field = field_grown.reshape(illum, 2, rows + 2 * reach, cols + reach)
    trans_reg = trans_grown.reshape(slices, 2, rows + 2 * reach, cols + reach)
    col_band = band[:, :, :width, :width]
    margins = [8 if (tall - 2 * HALF * (s + 1)) % 128 == 0 and s + 1 < slices else 0 for s in range(slices)]
    row_bands = [
        band[:, :, HALF * (s + 1) - margins[s]: tall - HALF * (s + 1) + margins[s], HALF * s: tall - HALF * s]
        for s in range(slices)
    ]

    last_band = jnp.where(wave == 0, col_band[:, :, :cols], col_band[:, :, reach:reach + cols])

    def depth_section(field):
        current = field
        for s in range(slices):
            if s and margins[s - 1]:
                current = current[:, :, margins[s - 1]: current.shape[2] - margins[s - 1]]
            moved = modulate(current, trans_reg[s, :, HALF * s: tall - HALF * s])
            rows_done = jnp.einsum(
                "dcab,icbj->idaj", row_bands[s], moved, precision=lax.Precision.HIGH
            )
            current = jnp.einsum(
                "dcyj,icxj->idxy",
                last_band if s == slices - 1 else col_band,
                rows_done,
                precision=lax.Precision.HIGH,
            )
        return current

    exits = jnp.zeros(incident.shape, jnp.float32)
    tiles = lax.axis_size("tile")
    spot = lambda t, d: t * depth_count + d
    ahead = range(depth_count - 1)
    own_pairs = [(spot(t, d), spot(t, d + 1)) for t in range(tiles) for d in ahead]
    prev_pairs = [(spot(t - 1, d), spot(t, d + 1)) for t in range(1, tiles) for d in ahead]
    next_pairs = [(spot(t + 1, d), spot(t, d + 1)) for t in range(tiles - 1) for d in ahead]
    field = first_field
    for step in range(depth_count):
        result = depth_section(field)
        exits = jnp.where(depth_index == step, result, exits)
        if step + 1 < depth_count:
            flat = result.reshape(2 * illum, rows, cols)
            grid = ("tile", "depth")
            from_prev = lax.ppermute(flat[:, rows - reach:], grid, prev_pairs)
            mine = lax.ppermute(flat, grid, own_pairs)
            from_next = lax.ppermute(flat[:, :reach], grid, next_pairs)
            field = widen(jnp.concatenate([from_prev, mine, from_next], axis=1), reach, (2 * illum,))[0].reshape(
                illum, 2, tall, width
            )
    return exits[None]


def solution(mesh):
    return jax.shard_map(
        per_device,
        mesh=mesh,
        in_specs=(
            P(None, None, ("groups", "tile"), "wave"),
            P("depth", ("groups", "tile"), "wave"),
            P("depth", ("groups", "tile"), "wave"),
            P(),
        ),
        out_specs=P("depth", None, None, ("groups", "tile"), "wave"),
        check_vma=False,
    )
```

```python
import jax
import jax.numpy as jnp
from jax import lax
from jax.sharding import PartitionSpec as P

TAPS = 33
HALF = 16


def toeplitz(kernel, size, shift):
    period = 2 * size
    gap = jnp.zeros((2, period - TAPS), jnp.float32)
    base = jnp.concatenate([kernel[:, shift:], gap, kernel[:, :shift]], axis=1)
    rolled = jnp.tile(base, (1, size))[:, : size * (period - 1)]
    bands = rolled.reshape(2, size, period - 1)[:, :, :size]
    band_real, band_imag = bands[0], bands[1]
    top = jnp.stack([band_real, -band_imag], axis=0)
    bottom = jnp.stack([band_imag, band_real], axis=0)
    return jnp.stack([top, bottom], axis=0)


def transmission(phase_part, absorb_part):
    amplitude = jnp.exp(-absorb_part.astype(jnp.float32))
    angle_part = phase_part.astype(jnp.float32)
    return jnp.stack([amplitude * jnp.cos(angle_part), amplitude * jnp.sin(angle_part)], axis=-3)


def modulate(field, trans):
    field_real = field[:, 0]
    field_imag = field[:, 1]
    return jnp.stack(
        [
            field_real * trans[0] - field_imag * trans[1],
            field_real * trans[1] + field_imag * trans[0],
        ],
        axis=1,
    )


def grow(stack, halo, splits, rider, needs=None):
    tiles = lax.axis_size("tile")
    rows, cols = stack.shape[-2], stack.shape[-1]
    needs = [halo] * stack.shape[0] if needs is None else needs
    slabs, places = [], []
    for c in sorted(range(len(needs)), key=lambda c: -needs[c]):
        for n, used in enumerate(slabs):
            if used + needs[c] <= halo:
                places.append((c, n, used))
                slabs[n] += needs[c]
                break
        else:
            places.append((c, len(slabs), 0))
            slabs.append(needs[c])

    def pack(take):
        bins = [[] for _ in slabs]
        for c, n, _ in places:
            bins[n].append(take(c))
        return jnp.stack([
            jnp.concatenate(b + [jnp.zeros((halo - used, cols), stack.dtype)] * (used < halo), axis=0)
            for b, used in zip(bins, slabs)
        ])

    sent_prev = pack(lambda c: stack[c, rows - needs[c]:])
    sent_next = pack(lambda c: stack[c, :needs[c]])
    from_prev = lax.ppermute(sent_prev, "tile", [(i, i + 1) for i in range(tiles - 1)])
    from_next = lax.ppermute(sent_next, "tile", [(i + 1, i) for i in range(tiles - 1)])
    columns = [None] * len(needs)
    for c, n, at in places:
        gap = [jnp.zeros((halo - needs[c], cols), stack.dtype)] * (needs[c] < halo)
        columns[c] = jnp.concatenate(
            gap + [from_prev[n, at:at + needs[c]], stack[c], from_next[n, at:at + needs[c]]] + gap,
            axis=0,
        )
    tall = jnp.stack(columns)
    rider, tall = lax.optimization_barrier((rider, tall))
    return widen(tall, halo, splits), rider


def widen(tall, halo, splits):
    wave = lax.axis_index("wave")
    count, cols = tall.shape[0], tall.shape[-1]
    if 2 * halo == cols:
        if count % 2:
            tall = jnp.concatenate([tall, jnp.zeros_like(tall[:1])])
        half = tall.shape[0] // 2
        slabs = jnp.where(
            wave == 0,
            jnp.concatenate([tall[:half, :, halo:], tall[half:, :, halo:]], axis=-1),
            jnp.concatenate([tall[:half, :, :halo], tall[half:, :, :halo]], axis=-1),
        )
        got = lax.ppermute(slabs, "wave", [(0, 1), (1, 0)])
        parts = jnp.concatenate([got[..., :halo], got[..., halo:]], axis=0)
    else:
        got = lax.ppermute(tall, "wave", [(0, 1), (1, 0)])
        parts = jnp.where(wave == 0, got[..., :halo], got[..., cols - halo:])
    out, start = [], 0
    for size in splits:
        own, part = tall[start:start + size], parts[start:start + size]
        start += size
        left = jnp.concatenate([own, part], axis=-1)
        right = jnp.concatenate([part, own], axis=-1)
        out.append(jnp.where(wave == 0, left, right))
    return out


def per_device(incident, phase_shift, absorption, fir_taps):
    kernel = fir_taps / jnp.sqrt(jnp.sum(fir_taps * fir_taps) + 1e-06)
    depth_index = lax.axis_index("depth")
    depth_count = lax.axis_size("depth")
    wave = lax.axis_index("wave")
    slices = phase_shift.shape[0]
    rows, cols = incident.shape[2], incident.shape[3]
    reach = HALF * slices
    assert reach <= rows and reach <= cols

    trans_own = transmission(phase_shift, absorption)
    illum = incident.shape[0]
    width = cols + reach
    tall = rows + 2 * reach
    band = toeplitz(kernel, max(tall, width), HALF)
    first_moved = modulate(incident, trans_own[0])
    (moved_grown, trans_grown), band = grow(
        jnp.concatenate([first_moved.reshape(2 * illum, rows, cols), trans_own[1:].reshape(2 * slices - 2, rows, cols)]),
        reach,
        (2 * illum, 2 * slices - 2),
        band,
        [reach] * (2 * illum) + [reach - HALF * s for s in range(1, slices) for _ in range(2)],
    )
    first_field = moved_grown.reshape(illum, 2, tall, width)
    trans_rest = trans_grown.reshape(slices - 1, 2, tall, width)
    col_band = band[:, :, :width, :width]
    margins = [8 if (tall - 2 * HALF * (s + 1)) % 128 == 0 and s + 1 < slices else 0 for s in range(slices)]
    row_bands = [
        band[:, :, HALF * (s + 1) - margins[s]: tall - HALF * (s + 1) + margins[s], HALF * s: tall - HALF * s]
        for s in range(slices)
    ]

    last_band = jnp.where(wave == 0, col_band[:, :, :cols], col_band[:, :, reach:reach + cols])

    def depth_section(field, trans_first, late=None):
        current = field
        for s in range(slices):
            if s and margins[s - 1]:
                current = current[:, :, margins[s - 1]: current.shape[2] - margins[s - 1]]
            if s:
                moved = modulate(current, trans_rest[s - 1, :, HALF * s: tall - HALF * s])
            elif trans_first is None:
                moved = current
            else:
                moved = modulate(current, trans_first)
            rows_done = jnp.einsum(
                "dcab,icbj->idaj", row_bands[s], moved, precision=lax.Precision.HIGH
            )
            current = jnp.einsum(
                "dcyj,icxj->idxy",
                last_band if s == slices - 1 else col_band,
                rows_done,
                precision=lax.Precision.HIGH,
            )
            if s == 0 and late is not None:
                current, late = lax.optimization_barrier((current, late))
                (late,), _ = grow(late, reach, (2,), jnp.zeros((), jnp.float32))
        return current, late

    exits = jnp.zeros(incident.shape, jnp.float32)
    tiles = lax.axis_size("tile")
    spot = lambda t, d: t * depth_count + d
    ahead = range(depth_count - 1)
    own_pairs = [(spot(t, d), spot(t, d + 1)) for t in range(tiles) for d in ahead]
    prev_pairs = [(spot(t - 1, d), spot(t, d + 1)) for t in range(1, tiles) for d in ahead]
    next_pairs = [(spot(t + 1, d), spot(t, d + 1)) for t in range(tiles - 1) for d in ahead]
    field, trans_first, late = first_field, None, trans_own[0]
    for step in range(depth_count):
        result, late = depth_section(field, trans_first, late)
        exits = jnp.where(depth_index == step, result, exits)
        if step + 1 < depth_count:
            if late is not None:
                trans_first, late = late, None
            flat = result.reshape(2 * illum, rows, cols)
            grid = ("tile", "depth")
            from_prev = lax.ppermute(flat[:, rows - reach:], grid, prev_pairs)
            mine = lax.ppermute(flat, grid, own_pairs)
            from_next = lax.ppermute(flat[:, :reach], grid, next_pairs)
            field = widen(jnp.concatenate([from_prev, mine, from_next], axis=1), reach, (2 * illum,))[0].reshape(
                illum, 2, tall, width
            )
    return exits[None]


def solution(mesh):
    return jax.shard_map(
        per_device,
        mesh=mesh,
        in_specs=(
            P(None, None, ("groups", "tile"), "wave"),
            P("depth", ("groups", "tile"), "wave"),
            P("depth", ("groups", "tile"), "wave"),
            P(),
        ),
        out_specs=P("depth", None, None, ("groups", "tile"), "wave"),
        check_vma=False,
    )
```

```python
import jax
import jax.numpy as jnp
from jax import lax
from jax.sharding import PartitionSpec as P

TAPS = 33
HALF = 16


def toeplitz(kernel, size, shift):
    period = 2 * size
    gap = jnp.zeros((2, period - TAPS), jnp.float32)
    base = jnp.concatenate([kernel[:, shift:], gap, kernel[:, :shift]], axis=1)
    rolled = jnp.tile(base, (1, size))[:, : size * (period - 1)]
    bands = rolled.reshape(2, size, period - 1)[:, :, :size]
    band_real, band_imag = bands[0], bands[1]
    top = jnp.stack([band_real, -band_imag], axis=0)
    bottom = jnp.stack([band_imag, band_real], axis=0)
    return jnp.stack([top, bottom], axis=0)


def transmission(phase_part, absorb_part):
    amplitude = jnp.exp(-absorb_part.astype(jnp.float32))
    angle_part = phase_part.astype(jnp.float32)
    return jnp.stack([amplitude * jnp.cos(angle_part), amplitude * jnp.sin(angle_part)], axis=-3)


def modulate(field, trans):
    field_real = field[:, 0]
    field_imag = field[:, 1]
    return jnp.stack(
        [
            field_real * trans[0] - field_imag * trans[1],
            field_real * trans[1] + field_imag * trans[0],
        ],
        axis=1,
    )


def grow(stack, halo, splits, rider, needs=None):
    tiles = lax.axis_size("tile")
    rows, cols = stack.shape[-2], stack.shape[-1]
    needs = [halo] * stack.shape[0] if needs is None else needs
    slabs, places = [], []
    for c in sorted(range(len(needs)), key=lambda c: -needs[c]):
        for n, used in enumerate(slabs):
            if used + needs[c] <= halo:
                places.append((c, n, used))
                slabs[n] += needs[c]
                break
        else:
            places.append((c, len(slabs), 0))
            slabs.append(needs[c])

    def pack(take):
        bins = [[] for _ in slabs]
        for c, n, _ in places:
            bins[n].append(take(c))
        return jnp.stack([
            jnp.concatenate(b + [jnp.zeros((halo - used, cols), stack.dtype)] * (used < halo), axis=0)
            for b, used in zip(bins, slabs)
        ])

    sent_prev = pack(lambda c: stack[c, rows - needs[c]:])
    sent_next = pack(lambda c: stack[c, :needs[c]])
    from_prev = lax.ppermute(sent_prev, "tile", [(i, i + 1) for i in range(tiles - 1)])
    from_next = lax.ppermute(sent_next, "tile", [(i + 1, i) for i in range(tiles - 1)])
    columns = [None] * len(needs)
    for c, n, at in places:
        gap = [jnp.zeros((halo - needs[c], cols), stack.dtype)] * (needs[c] < halo)
        columns[c] = jnp.concatenate(
            gap + [from_prev[n, at:at + needs[c]], stack[c], from_next[n, at:at + needs[c]]] + gap,
            axis=0,
        )
    tall = jnp.stack(columns)
    early = pair_halves(stack, halo) if 2 * halo == cols else None
    rider, early, tall = lax.optimization_barrier((rider, early, tall))
    return widen(tall, halo, splits, early), rider


def pair_halves(block, halo):
    wave = lax.axis_index("wave")
    if block.shape[0] % 2:
        block = jnp.concatenate([block, jnp.zeros_like(block[:1])])
    half = block.shape[0] // 2
    return jnp.where(
        wave == 0,
        jnp.concatenate([block[:half, :, halo:], block[half:, :, halo:]], axis=-1),
        jnp.concatenate([block[:half, :, :halo], block[half:, :, :halo]], axis=-1),
    )


def widen(tall, halo, splits, early=None):
    wave = lax.axis_index("wave")
    count, cols = tall.shape[0], tall.shape[-1]
    if 2 * halo == cols:
        if early is None:
            slabs = pair_halves(tall, halo)
        else:
            lines = tall.shape[1]
            slabs = jnp.concatenate(
                [pair_halves(tall[:, :halo], halo), early, pair_halves(tall[:, lines - halo:], halo)],
                axis=1,
            )
        got = lax.ppermute(slabs, "wave", [(0, 1), (1, 0)])
        parts = jnp.concatenate([got[..., :halo], got[..., halo:]], axis=0)
    else:
        got = lax.ppermute(tall, "wave", [(0, 1), (1, 0)])
        parts = jnp.where(wave == 0, got[..., :halo], got[..., cols - halo:])
    out, start = [], 0
    for size in splits:
        own, part = tall[start:start + size], parts[start:start + size]
        start += size
        left = jnp.concatenate([own, part], axis=-1)
        right = jnp.concatenate([part, own], axis=-1)
        out.append(jnp.where(wave == 0, left, right))
    return out


def per_device(incident, phase_shift, absorption, fir_taps):
    kernel = fir_taps / jnp.sqrt(jnp.sum(fir_taps * fir_taps) + 1e-06)
    depth_index = lax.axis_index("depth")
    depth_count = lax.axis_size("depth")
    wave = lax.axis_index("wave")
    slices = phase_shift.shape[0]
    rows, cols = incident.shape[2], incident.shape[3]
    reach = HALF * slices
    assert reach <= rows and reach <= cols

    trans_own = transmission(phase_shift, absorption)
    illum = incident.shape[0]
    width = cols + reach
    tall = rows + 2 * reach
    band = toeplitz(kernel, max(tall, width), HALF)
    (field_grown, trans_grown), band = grow(
        jnp.concatenate([incident.reshape(2 * illum, rows, cols), trans_own.reshape(2 * slices, rows, cols)]),
        reach,
        (2 * illum, 2 * slices),
        band,
        [reach] * (2 * illum) + [reach - HALF * s for s in range(slices) for _ in range(2)],
    )
    first_field = field_grown.reshape(illum, 2, rows + 2 * reach, cols + reach)
    trans_reg = trans_grown.reshape(slices, 2, rows + 2 * reach, cols + reach)
    col_band = band[:, :, :width, :width]
    margins = [8 if (tall - 2 * HALF * (s + 1)) % 128 == 0 and s + 1 < slices else 0 for s in range(slices)]
    row_bands = [
        band[:, :, HALF * (s + 1) - margins[s]: tall - HALF * (s + 1) + margins[s], HALF * s: tall - HALF * s]
        for s in range(slices)
    ]

    last_band = jnp.where(wave == 0, col_band[:, :, :cols], col_band[:, :, reach:reach + cols])

    def depth_section(field):
        current = field
        for s in range(slices):
            if s and margins[s - 1]:
                current = current[:, :, margins[s - 1]: current.shape[2] - margins[s - 1]]
            moved = modulate(current, trans_reg[s, :, HALF * s: tall - HALF * s])
            rows_done = jnp.einsum(
                "dcab,icbj->idaj", row_bands[s], moved, precision=lax.Precision.HIGH
            )
            current = jnp.einsum(
                "dcyj,icxj->idxy",
                last_band if s == slices - 1 else col_band,
                rows_done,
                precision=lax.Precision.HIGH,
            )
        return current

    exits = jnp.zeros(incident.shape, jnp.float32)
    tiles = lax.axis_size("tile")
    spot = lambda t, d: t * depth_count + d
    ahead = range(depth_count - 1)
    own_pairs = [(spot(t, d), spot(t, d + 1)) for t in range(tiles) for d in ahead]
    prev_pairs = [(spot(t - 1, d), spot(t, d + 1)) for t in range(1, tiles) for d in ahead]
    next_pairs = [(spot(t + 1, d), spot(t, d + 1)) for t in range(tiles - 1) for d in ahead]
    field = first_field
    for step in range(depth_count):
        result = depth_section(field)
        exits = jnp.where(depth_index == step, result, exits)
        if step + 1 < depth_count:
            flat = result.reshape(2 * illum, rows, cols)
            grid = ("tile", "depth")
            from_prev = lax.ppermute(flat[:, rows - reach:], grid, prev_pairs)
            mine = lax.ppermute(flat, grid, own_pairs)
            from_next = lax.ppermute(flat[:, :reach], grid, next_pairs)
            field = widen(jnp.concatenate([from_prev, mine, from_next], axis=1), reach, (2 * illum,))[0].reshape(
                illum, 2, tall, width
            )
    return exits[None]


def solution(mesh):
    return jax.shard_map(
        per_device,
        mesh=mesh,
        in_specs=(
            P(None, None, ("groups", "tile"), "wave"),
            P("depth", ("groups", "tile"), "wave"),
            P("depth", ("groups", "tile"), "wave"),
            P(),
        ),
        out_specs=P("depth", None, None, ("groups", "tile"), "wave"),
        check_vma=False,
    )
```
